256 devices in a mesh: row: 64 (over z_hi, y, x), col: 4 (over z_lo, core).
Axes of the slice: x: 4, y: 4, z: 8 (z_hi: 4, z_lo: 2; z = z_hi * 2 + z_lo), core: 2. Of those that a mesh axis runs over, the one named last changes fastest.
Arguments:
- efield_x: float32 [256, 32, 512], P('row', 'col'), may hold values from -0.6 to 0.6
- efield_y: float32 [256, 32, 512], P('row', 'col'), may hold values from -0.6 to 0.6
- efield_z: float32 [256, 32, 512], P('row', 'col'), may hold values from -0.6 to 0.6
- hfield_x: float32 [256, 32, 512], P('row', 'col'), may hold values from -0.6 to 0.6
- hfield_y: float32 [256, 32, 512], P('row', 'col'), may hold values from -0.6 to 0.6
- hfield_z: float32 [256, 32, 512], P('row', 'col'), may hold values from -0.6 to 0.6
- permittivity: float32 [256, 32, 512], P('row', 'col'), may hold values from 1 to 4.4
- conductivity: float32 [256, 32, 512], P('row', 'col'), may hold values from 0.001 to 0.05
Outputs:
- next_ex: float32 [256, 32, 512], P('row', 'col')
- next_ey: float32 [256, 32, 512], P('row', 'col')
- next_ez: float32 [256, 32, 512], P('row', 'col')
- next_hx: float32 [256, 32, 512], P('row', 'col')
- next_hy: float32 [256, 32, 512], P('row', 'col')
- next_hz: float32 [256, 32, 512], P('row', 'col')
The draws below stay inside these ranges and needn't reach their ends.
All inputs are finite; a program needn't handle non-finite values.
Results may differ from the reference program's by a relative error of at most 0.0055.
Values sent between devices are 32-bit elements; how exact they have to be, the bound alone decides.
No kernel may reach another device: no remote copies, remote signals or barrier semaphores. Data moves between devices by JAX's collectives and lax.ppermute only.
A program may use at most 64 MiB of HBM per device.

```python
import math
import jax
import jax.numpy as jnp
from jax import lax

NX = 512
NY = 256
NZ = 32


def shard_levels(rng, dims, pieces, smallest, top_value):
    def one(position, parts):
        draws = jax.random.uniform(jax.random.fold_in(jax.random.fold_in(rng, 6), position), (parts,), jnp.float32, smallest / len(pieces), top_value / len(pieces))
        return jnp.repeat(jnp.exp(draws), dims[position] // parts).reshape((-1,) + (1,) * (len(dims) - position - 1))

    factor_of = one(*pieces[0])
    for cut in pieces[1:]:
        factor_of = factor_of * one(*cut)
    return factor_of


def centred(rng, shape, width, reach, shards=(), held_as=jnp.bfloat16):
    array = jax.random.normal(rng, shape, jnp.float32) * width
    if len(shards) > 0:
        array = shard_levels(rng, shape, shards, -0.22, 0.18) * array
    return jnp.clip(array, min=-reach, max=reach).astype(held_as)


def setup_inputs(seed: int = 0) -> dict:
    key_list = jax.random.split(jax.random.key(seed), 9)
    return {
        "efield_x": centred(key_list[0], (NY, NZ, NX), 0.1, 0.6, ((0, 64), (1, 4)), jnp.float32),
        "efield_y": centred(key_list[1], (NY, NZ, NX), 0.1, 0.6, ((0, 64), (1, 4)), jnp.float32),
        "efield_z": centred(key_list[2], (NY, NZ, NX), 0.1, 0.6, ((0, 64), (1, 4)), jnp.float32),
        "hfield_x": centred(key_list[3], (NY, NZ, NX), 0.1, 0.6, ((0, 64), (1, 4)), jnp.float32),
        "hfield_y": centred(key_list[4], (NY, NZ, NX), 0.1, 0.6, ((0, 64), (1, 4)), jnp.float32),
        "hfield_z": centred(key_list[5], (NY, NZ, NX), 0.1, 0.6, ((0, 64), (1, 4)), jnp.float32),
        "permittivity": jnp.clip(jnp.exp(math.log(4.4) - 1.4816046 * jax.random.uniform(key_list[6], (NY, NZ, NX), jnp.float32) ** shard_levels(key_list[6], (NY, NZ, NX), ((0, 64), (1, 4)), -0.2, 0.2)), 1.0, 4.4),
        "conductivity": jnp.clip(jnp.exp(math.log(0.05) - 3.912023 * jax.random.uniform(key_list[7], (NY, NZ, NX), jnp.float32) ** shard_levels(key_list[7], (NY, NZ, NX), ((0, 64), (1, 4)), -0.2, 0.2)), 0.001, 0.05),
    }


HALF_STEP = 30.0


def shifted(values, stride, line_axis, filler, forward):
    length = values.shape[line_axis]
    padding = jnp.full_like(lax.slice_in_dim(values, 0, stride, axis=line_axis), filler)
    if forward:
        return jnp.concatenate([lax.slice_in_dim(values, stride, length, axis=line_axis), padding], line_axis)
    return jnp.concatenate([padding, lax.slice_in_dim(values, 0, length - stride, axis=line_axis)], line_axis)


def diff_up(values, line_axis):
    return shifted(values, 1, line_axis, 0.0, True) - values


def diff_down(values, line_axis):
    return values - shifted(values, 1, line_axis, 0.0, False)


def reduce_lines(sub_diag, main_diag, super_diag, source, line_axis):
    length = source.shape[line_axis]
    stride = 1
    while stride < length:
        sub_lo = shifted(sub_diag, stride, line_axis, 0.0, False)
        mid_lo = shifted(main_diag, stride, line_axis, 1.0, False)
        sup_lo = shifted(super_diag, stride, line_axis, 0.0, False)
        src_lo = shifted(source, stride, line_axis, 0.0, False)
        sub_hi = shifted(sub_diag, stride, line_axis, 0.0, True)
        mid_hi = shifted(main_diag, stride, line_axis, 1.0, True)
        sup_hi = shifted(super_diag, stride, line_axis, 0.0, True)
        src_hi = shifted(source, stride, line_axis, 0.0, True)
        ratio_lo = sub_diag / mid_lo
        ratio_hi = super_diag / mid_hi
        sub_diag = -sub_lo * ratio_lo
        super_diag = -sup_hi * ratio_hi
        main_diag = main_diag - sup_lo * ratio_lo - sub_hi * ratio_hi
        source = source - src_lo * ratio_lo - src_hi * ratio_hi
        stride = stride * 2
    return source / main_diag


def line_flags(length, line_axis, rank):
    iota_shape = [1] * rank
    iota_shape[line_axis] = length
    where_line = lax.broadcasted_iota(jnp.int32, tuple(iota_shape), line_axis)
    return where_line == 0, where_line == length - 1


def line_system(coupling, is_first, is_final):
    sub_diag = jnp.where(is_first, 0.0, -coupling)
    main_diag = jnp.where(is_first, 1.0 + coupling, 1.0 + 2.0 * coupling)
    super_diag = jnp.where(is_final, 0.0, -coupling)
    return sub_diag, main_diag, super_diag


def solve_local(source, coupling, line_axis):
    is_first, is_final = line_flags(source.shape[line_axis], line_axis, source.ndim)
    sub_diag, main_diag, super_diag = line_system(coupling, is_first, is_final)
    return reduce_lines(sub_diag, main_diag, super_diag, source, line_axis)


def reference(efield_x, efield_y, efield_z, hfield_x, hfield_y, hfield_z, permittivity, conductivity):
    damping = conductivity * HALF_STEP / (2.0 * permittivity)
    keep_coef = (1.0 - damping) / (1.0 + damping)
    drive_coef = HALF_STEP / (permittivity * (1.0 + damping))
    coupling = drive_coef * HALF_STEP
    source_x = keep_coef * efield_x + drive_coef * (diff_down(hfield_z, 0) - diff_down(hfield_y, 1) - HALF_STEP * diff_down(diff_up(efield_y, 2), 0))
    source_y = keep_coef * efield_y + drive_coef * (diff_down(hfield_x, 1) - diff_down(hfield_z, 2) - HALF_STEP * diff_down(diff_up(efield_z, 0), 1))
    source_z = keep_coef * efield_z + drive_coef * (diff_down(hfield_y, 2) - diff_down(hfield_x, 0) - HALF_STEP * diff_down(diff_up(efield_x, 1), 2))
    half_ex = solve_local(source_x, coupling, 0)
    half_ey = solve_local(source_y, coupling, 1)
    half_ez = solve_local(source_z, coupling, 2)
    half_hx = hfield_x + HALF_STEP * (diff_up(half_ey, 1) - diff_up(efield_z, 0))
    half_hy = hfield_y + HALF_STEP * (diff_up(half_ez, 2) - diff_up(efield_x, 1))
    half_hz = hfield_z + HALF_STEP * (diff_up(half_ex, 0) - diff_up(efield_y, 2))
    second_x = keep_coef * half_ex + drive_coef * (diff_down(half_hz, 0) - diff_down(half_hy, 1) - HALF_STEP * diff_down(diff_up(half_ez, 2), 1))
    second_y = keep_coef * half_ey + drive_coef * (diff_down(half_hx, 1) - diff_down(half_hz, 2) - HALF_STEP * diff_down(diff_up(half_ex, 0), 2))
    second_z = keep_coef * half_ez + drive_coef * (diff_down(half_hy, 2) - diff_down(half_hx, 0) - HALF_STEP * diff_down(diff_up(half_ey, 1), 0))
    next_ex = solve_local(second_x, coupling, 1)
    next_ey = solve_local(second_y, coupling, 2)
    next_ez = solve_local(second_z, coupling, 0)
    next_hx = half_hx + HALF_STEP * (diff_up(half_ey, 1) - diff_up(next_ez, 0))
    next_hy = half_hy + HALF_STEP * (diff_up(half_ez, 2) - diff_up(next_ex, 1))
    next_hz = half_hz + HALF_STEP * (diff_up(half_ex, 0) - diff_up(next_ey, 2))
    return (next_ex, next_ey, next_ez, next_hx, next_hy, next_hz)
```

```python
import jax
import jax.numpy as jnp
from jax import lax
from jax.sharding import PartitionSpec as P

HALF_STEP = 30.0


def with_halo(cells, sides, width):
    for axis, dim in sides:
        count = lax.axis_size(axis)
        ends = count - 1
        head = lax.slice_in_dim(cells, 0, width, axis=dim)
        tail = lax.slice_in_dim(cells, cells.shape[dim] - width, cells.shape[dim], axis=dim)
        cells = jnp.concatenate(
            [
                lax.ppermute(tail, axis, [(i, (i + 1) % count) for i in range(ends)]),
                cells,
                lax.ppermute(head, axis, [((i + 1) % count, i) for i in range(ends)]),
            ],
            axis=dim,
        )
    return cells


def shifted(values, stride, line_axis, filler, forward):
    length = values.shape[line_axis]
    padding = jnp.full_like(lax.slice_in_dim(values, 0, stride, axis=line_axis), filler)
    if forward:
        return jnp.concatenate(
            [lax.slice_in_dim(values, stride, length, axis=line_axis), padding], line_axis
        )
    return jnp.concatenate(
        [padding, lax.slice_in_dim(values, 0, length - stride, axis=line_axis)], line_axis
    )


def diff_up(values, line_axis):
    return shifted(values, 1, line_axis, 0.0, True) - values


def diff_down(values, line_axis):
    return values - shifted(values, 1, line_axis, 0.0, False)


def reduce_lines(sub_diag, main_diag, super_diag, source, line_axis):
    length = source.shape[line_axis]
    stride = 1
    while stride < length:
        sub_lo = shifted(sub_diag, stride, line_axis, 0.0, False)
        mid_lo = shifted(main_diag, stride, line_axis, 1.0, False)
        sup_lo = shifted(super_diag, stride, line_axis, 0.0, False)
        src_lo = shifted(source, stride, line_axis, 0.0, False)
        sub_hi = shifted(sub_diag, stride, line_axis, 0.0, True)
        mid_hi = shifted(main_diag, stride, line_axis, 1.0, True)
        sup_hi = shifted(super_diag, stride, line_axis, 0.0, True)
        src_hi = shifted(source, stride, line_axis, 0.0, True)
        ratio_lo = sub_diag / mid_lo
        ratio_hi = super_diag / mid_hi
        sub_diag = -sub_lo * ratio_lo
        super_diag = -sup_hi * ratio_hi
        main_diag = main_diag - sup_lo * ratio_lo - sub_hi * ratio_hi
        source = source - src_lo * ratio_lo - src_hi * ratio_hi
        stride = stride * 2
    return source / main_diag


def line_flags(length, line_axis, rank):
    iota_shape = [1] * rank
    iota_shape[line_axis] = length
    where_line = lax.broadcasted_iota(jnp.int32, tuple(iota_shape), line_axis)
    return (where_line == 0, where_line == length - 1)


def line_system(coupling, is_first, is_final):
    sub_diag = jnp.where(is_first, 0.0, -coupling)
    main_diag = jnp.where(is_first, 1.0 + coupling, 1.0 + 2.0 * coupling)
    super_diag = jnp.where(is_final, 0.0, -coupling)
    return (sub_diag, main_diag, super_diag)


def solve_local(source, coupling, line_axis):
    is_first, is_final = line_flags(source.shape[line_axis], line_axis, source.ndim)
    sub_diag, main_diag, super_diag = line_system(coupling, is_first, is_final)
    return reduce_lines(sub_diag, main_diag, super_diag, source, line_axis)


def inside_mask(count_y, count_z):
    pos_y = (
        lax.axis_index("row") * count_y
        + lax.broadcasted_iota(jnp.int32, (count_y + 2, 1, 1), 0)
        - 1
    )
    pos_z = (
        lax.axis_index("col") * count_z
        + lax.broadcasted_iota(jnp.int32, (1, count_z + 2, 1), 1)
        - 1
    )
    inside = (
        (pos_y >= 0)
        & (pos_y < count_y * lax.axis_size("row"))
        & (pos_z >= 0)
        & (pos_z < count_z * lax.axis_size("col"))
    )
    return inside


class RowSystem:
    def __init__(self, coupling):
        count = coupling.shape[0]
        self.count = count
        row_index = lax.axis_index("row")
        is_first, is_final = line_flags(count, 0, 3)
        is_first = jnp.logical_and(is_first, row_index == 0)
        is_final = jnp.logical_and(is_final, row_index == lax.axis_size("row") - 1)
        sub, main, sup = line_system(coupling, is_first, is_final)
        self.sub, self.main, self.sup = sub, main, sup
        fwd_sub = [None] * count
        fwd_sup = [None] * count
        pivot = [None] * count
        pivot[1] = main[1]
        fwd_sub[1] = sub[1] / main[1]
        fwd_sup[1] = sup[1] / main[1]
        for level in range(2, count - 1):
            pivot[level] = main[level] - sub[level] * fwd_sup[level - 1]
            fwd_sub[level] = -sub[level] * fwd_sub[level - 1] / pivot[level]
            fwd_sup[level] = sup[level] / pivot[level]
        bwd_sub = [None] * count
        bwd_sup = [None] * count
        bwd_sub[count - 2] = fwd_sub[count - 2]
        bwd_sup[count - 2] = fwd_sup[count - 2]
        for level in range(count - 3, 0, -1):
            bwd_sub[level] = fwd_sub[level] - fwd_sup[level] * bwd_sub[level + 1]
            bwd_sup[level] = -fwd_sup[level] * bwd_sup[level + 1]
        last = count - 1
        self.pivot, self.fwd_sub, self.fwd_sup = pivot, fwd_sub, fwd_sup
        self.bwd_sub, self.bwd_sup = bwd_sub, bwd_sup
        self.head = [sub[0], main[0] - sup[0] * bwd_sub[1], -sup[0] * bwd_sup[1]]
        self.tail = [
            -sub[last] * fwd_sub[last - 1],
            main[last] - sub[last] * fwd_sup[last - 1],
            sup[last],
        ]

    def reduce_source(self, source):
        count = self.count
        sub = self.sub
        fwd_src = [None] * count
        fwd_src[1] = source[1] / self.pivot[1]
        for level in range(2, count - 1):
            fwd_src[level] = (source[level] - sub[level] * fwd_src[level - 1]) / self.pivot[level]
        bwd_src = [None] * count
        bwd_src[count - 2] = fwd_src[count - 2]
        for level in range(count - 3, 0, -1):
            bwd_src[level] = fwd_src[level] - self.fwd_sup[level] * bwd_src[level + 1]
        last = count - 1
        head_src = source[0] - self.sup[0] * bwd_src[1]
        tail_src = source[last] - sub[last] * fwd_src[last - 1]
        return bwd_src, head_src, tail_src

    def expand(self, bwd_src, first_vals, final_vals):
        rows = [first_vals]
        for level in range(1, self.count - 1):
            rows.append(
                bwd_src[level] - self.bwd_sub[level] * first_vals - self.bwd_sup[level] * final_vals
            )
        rows.append(final_vals)
        return rows


def to_solver(planes, parts):
    lead = planes.shape[:-2]
    count_z, count_x = planes.shape[-2:]
    per_z = parts // count_z
    width = count_x // per_z
    split = planes.reshape(lead + (count_z, per_z, width))
    rank = len(lead)
    order = (rank, rank + 1) + tuple(range(rank)) + (rank + 2,)
    split = jnp.transpose(split, order)
    return split.reshape((parts,) + lead + (width,))


def from_solver(chunks, count_z, count_x):
    parts, k, width = chunks.shape
    per_z = parts // count_z
    split = chunks.reshape((count_z, per_z, k, width))
    split = jnp.transpose(split, (2, 0, 1, 3))
    return split.reshape((k, count_z, count_x))


def reduced_solve(matrix, rhs, want_prev):
    solved = reduce_lines(matrix[0], matrix[1], matrix[2], rhs, 0)
    parts = solved.shape[0] // 2
    pairs = solved.reshape((parts, 2) + solved.shape[1:])
    heads = pairs[:, 0]
    tails = pairs[:, 1]
    zero = jnp.zeros_like(heads[:1])
    next_heads = jnp.concatenate([heads[1:], zero], 0)
    outs = [heads, tails, next_heads]
    if want_prev:
        outs.append(jnp.concatenate([zero, tails[:-1]], 0))
    return jnp.stack(outs, 1)


def on_device(
    efield_x, efield_y, efield_z, hfield_x, hfield_y, hfield_z, permittivity, conductivity
):
    count_y = efield_x.shape[0]
    count_z = efield_x.shape[1]
    count_x = efield_x.shape[2]
    rows = lax.axis_size("row")
    col_index = lax.axis_index("col")

    ext = with_halo(
        jnp.stack(
            [efield_x, efield_y, efield_z, hfield_x, hfield_y, hfield_z, permittivity, conductivity]
        ),
        (("row", 1), ("col", 2)),
        1,
    )
    inside = inside_mask(count_y, count_z)
    ex_e, ey_e, ez_e = ext[0], ext[1], ext[2]
    hx_e, hy_e, hz_e = ext[3], ext[4], ext[5]
    eps_e = jnp.where(inside, ext[6], 1.0)
    sig_e = jnp.where(inside, ext[7], 0.0)
    damping = sig_e * HALF_STEP / (2.0 * eps_e)
    keep_e = (1.0 - damping) / (1.0 + damping)
    drive_e = HALF_STEP / (eps_e * (1.0 + damping))
    coup_e = drive_e * HALF_STEP

    ys = slice(1, count_y + 1)
    zs = slice(1, count_z + 1)
    keep = keep_e[ys, zs]
    drive = drive_e[ys, zs]
    coupling = coup_e[ys, zs]

    dpx_ey = diff_up(ey_e[0 : count_y + 1, zs], 2)
    source_x = keep * efield_x + drive * (
        (hz_e[ys, zs] - hz_e[0:count_y, zs])
        - (hy_e[ys, zs] - hy_e[ys, 0:count_z])
        - HALF_STEP * (dpx_ey[1:] - dpx_ey[:-1])
    )
    ya = slice(0, count_y + 1)
    dpy_ez = ez_e[1 : count_y + 2, 0 : count_z + 1] - ez_e[0 : count_y + 1, 0 : count_z + 1]
    source_y = keep_e[ya, zs] * ey_e[ya, zs] + drive_e[ya, zs] * (
        (hx_e[ya, zs] - hx_e[ya, 0:count_z])
        - diff_down(hz_e[ya, zs], 2)
        - HALF_STEP * (dpy_ez[:, 1:] - dpy_ez[:, :-1])
    )
    za = slice(0, count_z + 1)
    dpz_ex = ex_e[ys, 1 : count_z + 2] - ex_e[ys, 0 : count_z + 1]
    source_z = keep_e[ys, za] * ez_e[ys, za] + drive_e[ys, za] * (
        diff_down(hy_e[ys, za], 2)
        - (hx_e[ys, za] - hx_e[0:count_y, za])
        - HALF_STEP * diff_down(dpz_ex, 2)
    )

    gathered = lax.all_gather(
        jnp.stack([source_y, coup_e[ya, zs]]), "col", axis=2, tiled=True
    )
    coup_full = gathered[1]
    half_ey_full = solve_local(gathered[0], coup_full, 1)
    pos_y = (
        lax.axis_index("row") * count_y
        + lax.broadcasted_iota(jnp.int32, (count_y + 1, 1, 1), 0)
        - 1
    )
    half_ey_full = jnp.where(pos_y >= 0, half_ey_full, 0.0)
    padded = jnp.pad(half_ey_full, ((0, 0), (1, 1), (0, 0)))
    half_ey_e = lax.dynamic_slice_in_dim(padded, col_index * count_z, count_z + 2, axis=1)

    half_ez_e = solve_local(source_z, coup_e[ys, za], 2)
    half_ez_e = jnp.where(inside[ys, za], half_ez_e, 0.0)

    system = RowSystem(coupling)
    bwd_src, head_src, tail_src = system.reduce_source(source_x)
    parts = rows
    payload = jnp.stack(
        [
            jnp.stack(system.head + [head_src]),
            jnp.stack(system.tail + [tail_src]),
        ],
        1,
    )
    payload = to_solver(payload, parts)
    received = lax.all_to_all(payload, "row", split_axis=0, concat_axis=0, tiled=True)
    width = received.shape[-1]
    received = jnp.transpose(received, (1, 0, 2, 3)).reshape((4, parts * 2, width))
    matrix = received[:3]
    answer = reduced_solve(matrix, received[3], True)
    back = lax.all_to_all(answer, "row", split_axis=0, concat_axis=0, tiled=True)
    bounds = from_solver(back, count_z, count_x)
    half_ex_rows = system.expand(bwd_src, bounds[0], bounds[1])
    half_ex_e = jnp.stack([bounds[3]] + half_ex_rows + [bounds[2]])

    inside_e = inside
    half_hz_e = hz_e[ya, zs] + HALF_STEP * (
        (half_ex_e[1:] - half_ex_e[:-1]) - diff_up(ey_e[ya, zs], 2)
    )
    half_hz_e = jnp.where(inside_e[ya, zs], half_hz_e, 0.0)
    half_hy_e = hy_e[ys, za] + HALF_STEP * (diff_up(half_ez_e, 2) - dpz_ex)
    half_hy_e = jnp.where(inside_e[ys, za], half_hy_e, 0.0)
    dz_half_ey = half_ey_e[:, 1:] - half_ey_e[:, :-1]
    half_hx_e = hx_e[ya, za] + HALF_STEP * (dz_half_ey[:, 0 : count_z + 1] - dpy_ez)
    half_hx_e = jnp.where(inside_e[ya, za], half_hx_e, 0.0)

    half_ex = half_ex_e[1 : count_y + 1]
    half_ey = half_ey_e[1 : count_y + 1, 1 : count_z + 1]
    half_ez = half_ez_e[:, 1:]
    dx_half_ez = diff_up(half_ez_e, 2)
    dy_half_ex = half_ex_e[2:] - half_ex_e[1:-1]
    second_x = keep * half_ex + drive * (
        (half_hz_e[1:] - half_hz_e[:-1])
        - (half_hy_e[:, 1:] - half_hy_e[:, :-1])
        - HALF_STEP * (dx_half_ez[:, 1:] - dx_half_ez[:, :-1])
    )
    second_y = keep * half_ey + drive * (
        (half_hx_e[1:, 1:] - half_hx_e[1:, :-1])
        - diff_down(half_hz_e[1:], 2)
        - HALF_STEP * diff_down(dy_half_ex, 2)
    )
    dz_ey_own = dz_half_ey[:, 1 : count_z + 1]
    second_z = keep * half_ez + drive * (
        diff_down(half_hy_e[:, 1:], 2)
        - (half_hx_e[1:, 1:] - half_hx_e[:-1, 1:])
        - HALF_STEP * (dz_ey_own[1:] - dz_ey_own[:-1])
    )

    second_full = lax.all_gather(second_x, "col", axis=1, tiled=True)
    next_ex_full = solve_local(second_full, coup_full[1:], 1)
    padded = jnp.pad(next_ex_full, ((0, 0), (0, 1), (0, 0)))
    next_ex_e = lax.dynamic_slice_in_dim(padded, col_index * count_z, count_z + 1, axis=1)
    next_ex = next_ex_e[:, :-1]

    next_ey = solve_local(second_y, coupling, 2)

    bwd_src, head_src, tail_src = system.reduce_source(second_z)
    payload = to_solver(jnp.stack([head_src, tail_src]), parts)
    received = lax.all_to_all(payload, "row", split_axis=0, concat_axis=0, tiled=True)
    answer = reduced_solve(matrix, received.reshape((parts * 2, width)), False)
    back = lax.all_to_all(answer, "row", split_axis=0, concat_axis=0, tiled=True)
    bounds = from_solver(back, count_z, count_x)
    next_ez_rows = system.expand(bwd_src, bounds[0], bounds[1])
    next_ez = jnp.stack(next_ez_rows)
    next_ez_e = jnp.stack(next_ez_rows + [bounds[2]])

    next_hx = half_hx_e[1:, 1:] + HALF_STEP * (
        dz_ey_own[1:] - (next_ez_e[1:] - next_ez_e[:-1])
    )
    next_hy = half_hy_e[:, 1:] + HALF_STEP * (
        dx_half_ez[:, 1:] - (next_ex_e[:, 1:] - next_ex_e[:, :-1])
    )
    next_hz = half_hz_e[1:] + HALF_STEP * (dy_half_ex - diff_up(next_ey, 2))
    return (next_ex, next_ey, next_ez, next_hx, next_hy, next_hz)


def solution(mesh):
    spec = P("row", "col", None)
    return jax.shard_map(
        on_device,
        mesh=mesh,
        in_specs=(spec,) * 8,
        out_specs=(spec,) * 6,
        check_vma=False,
    )
```

```python
import jax
import jax.numpy as jnp
from jax import lax
from jax.sharding import PartitionSpec as P

HALF_STEP = 30.0


def with_halo(cells, sides, width):
    for axis, dim in sides:
        count = lax.axis_size(axis)
        ends = count - 1
        head = lax.slice_in_dim(cells, 0, width, axis=dim)
        tail = lax.slice_in_dim(cells, cells.shape[dim] - width, cells.shape[dim], axis=dim)
        cells = jnp.concatenate(
            [
                lax.ppermute(tail, axis, [(i, (i + 1) % count) for i in range(ends)]),
                cells,
                lax.ppermute(head, axis, [((i + 1) % count, i) for i in range(ends)]),
            ],
            axis=dim,
        )
    return cells


def shifted(values, stride, line_axis, filler, forward):
    length = values.shape[line_axis]
    padding = jnp.full_like(lax.slice_in_dim(values, 0, stride, axis=line_axis), filler)
    if forward:
        return jnp.concatenate(
            [lax.slice_in_dim(values, stride, length, axis=line_axis), padding], line_axis
        )
    return jnp.concatenate(
        [padding, lax.slice_in_dim(values, 0, length - stride, axis=line_axis)], line_axis
    )


def diff_up(values, line_axis):
    return shifted(values, 1, line_axis, 0.0, True) - values


def diff_down(values, line_axis):
    return values - shifted(values, 1, line_axis, 0.0, False)


def reduce_lines(sub_diag, main_diag, super_diag, source, line_axis):
    length = source.shape[line_axis]
    stride = 1
    while stride < length:
        sub_lo = shifted(sub_diag, stride, line_axis, 0.0, False)
        mid_lo = shifted(main_diag, stride, line_axis, 1.0, False)
        sup_lo = shifted(super_diag, stride, line_axis, 0.0, False)
        src_lo = shifted(source, stride, line_axis, 0.0, False)
        sub_hi = shifted(sub_diag, stride, line_axis, 0.0, True)
        mid_hi = shifted(main_diag, stride, line_axis, 1.0, True)
        sup_hi = shifted(super_diag, stride, line_axis, 0.0, True)
        src_hi = shifted(source, stride, line_axis, 0.0, True)
        ratio_lo = sub_diag / mid_lo
        ratio_hi = super_diag / mid_hi
        sub_diag = -sub_lo * ratio_lo
        super_diag = -sup_hi * ratio_hi
        main_diag = main_diag - sup_lo * ratio_lo - sub_hi * ratio_hi
        source = source - src_lo * ratio_lo - src_hi * ratio_hi
        stride = stride * 2
    return source / main_diag


def line_flags(length, line_axis, rank):
    iota_shape = [1] * rank
    iota_shape[line_axis] = length
    where_line = lax.broadcasted_iota(jnp.int32, tuple(iota_shape), line_axis)
    return (where_line == 0, where_line == length - 1)


def line_system(coupling, is_first, is_final):
    sub_diag = jnp.where(is_first, 0.0, -coupling)
    main_diag = jnp.where(is_first, 1.0 + coupling, 1.0 + 2.0 * coupling)
    super_diag = jnp.where(is_final, 0.0, -coupling)
    return (sub_diag, main_diag, super_diag)


def solve_local(source, coupling, line_axis):
    is_first, is_final = line_flags(source.shape[line_axis], line_axis, source.ndim)
    sub_diag, main_diag, super_diag = line_system(coupling, is_first, is_final)
    return reduce_lines(sub_diag, main_diag, super_diag, source, line_axis)


def inside_mask(count_y, count_z):
    pos_y = (
        lax.axis_index("row") * count_y
        + lax.broadcasted_iota(jnp.int32, (count_y + 2, 1, 1), 0)
        - 1
    )
    pos_z = (
        lax.axis_index("col") * count_z
        + lax.broadcasted_iota(jnp.int32, (1, count_z + 2, 1), 1)
        - 1
    )
    inside = (
        (pos_y >= 0)
        & (pos_y < count_y * lax.axis_size("row"))
        & (pos_z >= 0)
        & (pos_z < count_z * lax.axis_size("col"))
    )
    return inside


class RowSystem:
    def __init__(self, coupling):
        count = coupling.shape[0]
        self.count = count
        row_index = lax.axis_index("row")
        is_first, is_final = line_flags(count, 0, 3)
        is_first = jnp.logical_and(is_first, row_index == 0)
        is_final = jnp.logical_and(is_final, row_index == lax.axis_size("row") - 1)
        sub, main, sup = line_system(coupling, is_first, is_final)
        self.sub, self.main, self.sup = sub, main, sup
        fwd_sub = [None] * count
        fwd_sup = [None] * count
        pivot = [None] * count
        pivot[1] = main[1]
        fwd_sub[1] = sub[1] / main[1]
        fwd_sup[1] = sup[1] / main[1]
        for level in range(2, count - 1):
            pivot[level] = main[level] - sub[level] * fwd_sup[level - 1]
            fwd_sub[level] = -sub[level] * fwd_sub[level - 1] / pivot[level]
            fwd_sup[level] = sup[level] / pivot[level]
        bwd_sub = [None] * count
        bwd_sup = [None] * count
        bwd_sub[count - 2] = fwd_sub[count - 2]
        bwd_sup[count - 2] = fwd_sup[count - 2]
        for level in range(count - 3, 0, -1):
            bwd_sub[level] = fwd_sub[level] - fwd_sup[level] * bwd_sub[level + 1]
            bwd_sup[level] = -fwd_sup[level] * bwd_sup[level + 1]
        last = count - 1
        self.pivot, self.fwd_sub, self.fwd_sup = pivot, fwd_sub, fwd_sup
        self.bwd_sub, self.bwd_sup = bwd_sub, bwd_sup
        self.head = [sub[0], main[0] - sup[0] * bwd_sub[1], -sup[0] * bwd_sup[1]]
        self.tail = [
            -sub[last] * fwd_sub[last - 1],
            main[last] - sub[last] * fwd_sup[last - 1],
            sup[last],
        ]

    def reduce_source(self, source):
        count = self.count
        sub = self.sub
        fwd_src = [None] * count
        fwd_src[1] = source[1] / self.pivot[1]
        for level in range(2, count - 1):
            fwd_src[level] = (source[level] - sub[level] * fwd_src[level - 1]) / self.pivot[level]
        bwd_src = [None] * count
        bwd_src[count - 2] = fwd_src[count - 2]
        for level in range(count - 3, 0, -1):
            bwd_src[level] = fwd_src[level] - self.fwd_sup[level] * bwd_src[level + 1]
        last = count - 1
        head_src = source[0] - self.sup[0] * bwd_src[1]
        tail_src = source[last] - sub[last] * fwd_src[last - 1]
        return bwd_src, head_src, tail_src

    def expand(self, bwd_src, first_vals, final_vals):
        rows = [first_vals]
        for level in range(1, self.count - 1):
            rows.append(
                bwd_src[level] - self.bwd_sub[level] * first_vals - self.bwd_sup[level] * final_vals
            )
        rows.append(final_vals)
        return rows


def to_solver(planes, parts):
    lead = planes.shape[:-2]
    count_z, count_x = planes.shape[-2:]
    per_z = parts // count_z
    width = count_x // per_z
    split = planes.reshape(lead + (count_z, per_z, width))
    rank = len(lead)
    order = (rank, rank + 1) + tuple(range(rank)) + (rank + 2,)
    split = jnp.transpose(split, order)
    return split.reshape((parts,) + lead + (width,))


def from_solver(chunks, count_z, count_x):
    parts, k, width = chunks.shape
    per_z = parts // count_z
    split = chunks.reshape((count_z, per_z, k, width))
    split = jnp.transpose(split, (2, 0, 1, 3))
    return split.reshape((k, count_z, count_x))


def reduced_solve(matrix, rhs, want_prev):
    solved = reduce_lines(matrix[0][None], matrix[1][None], matrix[2][None], rhs, 1)
    parts = solved.shape[1] // 2
    outs = []
    for one in range(solved.shape[0]):
        pairs = solved[one].reshape((parts, 2) + solved.shape[2:])
        heads = pairs[:, 0]
        tails = pairs[:, 1]
        zero = jnp.zeros_like(heads[:1])
        outs += [heads, tails]
    for one in range(solved.shape[0]):
        heads = outs[2 * one]
        outs.append(jnp.concatenate([heads[1:], zero], 0))
    outs.append(jnp.concatenate([zero, outs[1][:-1]], 0))
    return jnp.stack(outs, 1)


def field_halos(fields):
    rows = lax.axis_size("row")
    cols = lax.axis_size("col")
    down_rows = [(i, i + 1) for i in range(rows - 1)]
    up_rows = [(i + 1, i) for i in range(rows - 1)]
    down_cols = [(i, i + 1) for i in range(cols - 1)]
    up_cols = [(i + 1, i) for i in range(cols - 1)]
    from_prev = lax.ppermute(jnp.stack([f[-1:] for f in fields]), "row", down_rows)
    from_next = lax.ppermute(jnp.stack([f[:1] for f in fields]), "row", up_rows)
    ext_y = [
        jnp.concatenate([from_prev[k], f, from_next[k]], 0) for k, f in enumerate(fields)
    ]
    from_left = lax.ppermute(jnp.stack([e[:, -1:] for e in ext_y]), "col", down_cols)
    from_right = lax.ppermute(jnp.stack([e[:, :1] for e in ext_y]), "col", up_cols)
    return [
        jnp.concatenate([from_left[k], e, from_right[k]], 1) for k, e in enumerate(ext_y)
    ]


def on_device(
    efield_x, efield_y, efield_z, hfield_x, hfield_y, hfield_z, permittivity, conductivity
):
    count_y = efield_x.shape[0]
    count_z = efield_x.shape[1]
    count_x = efield_x.shape[2]
    rows = lax.axis_size("row")
    col_index = lax.axis_index("col")

    ext = field_halos(
        [efield_x, efield_y, efield_z, hfield_x, hfield_y, hfield_z, permittivity, conductivity]
    )
    inside = inside_mask(count_y, count_z)
    ex_e, ey_e, ez_e = ext[0], ext[1], ext[2]
    hx_e, hy_e, hz_e = ext[3], ext[4], ext[5]
    eps_e = jnp.where(inside, ext[6], 1.0)
    sig_e = jnp.where(inside, ext[7], 0.0)
    damping = sig_e * HALF_STEP / (2.0 * eps_e)
    keep_e = (1.0 - damping) / (1.0 + damping)
    drive_e = HALF_STEP / (eps_e * (1.0 + damping))
    coup_e = drive_e * HALF_STEP

    ys = slice(1, count_y + 1)
    zs = slice(1, count_z + 1)
    keep = keep_e[ys, zs]
    drive = drive_e[ys, zs]
    coupling = coup_e[ys, zs]

    dpx_ey = diff_up(ey_e[0 : count_y + 1, zs], 2)
    source_x = keep * efield_x + drive * (
        (hz_e[ys, zs] - hz_e[0:count_y, zs])
        - (hy_e[ys, zs] - hy_e[ys, 0:count_z])
        - HALF_STEP * (dpx_ey[1:] - dpx_ey[:-1])
    )
    ya = slice(0, count_y + 1)
    dpy_ez = ez_e[1 : count_y + 2, 0 : count_z + 1] - ez_e[0 : count_y + 1, 0 : count_z + 1]
    source_y = keep_e[ya, zs] * ey_e[ya, zs] + drive_e[ya, zs] * (
        (hx_e[ya, zs] - hx_e[ya, 0:count_z])
        - diff_down(hz_e[ya, zs], 2)
        - HALF_STEP * (dpy_ez[:, 1:] - dpy_ez[:, :-1])
    )
    za = slice(0, count_z + 1)
    dpz_ex = ex_e[ys, 1 : count_z + 2] - ex_e[ys, 0 : count_z + 1]
    source_z = keep_e[ys, za] * ez_e[ys, za] + drive_e[ys, za] * (
        diff_down(hy_e[ys, za], 2)
        - (hx_e[ys, za] - hx_e[0:count_y, za])
        - HALF_STEP * diff_down(dpz_ex, 2)
    )

    gathered = lax.all_gather(
        jnp.stack([source_y, coup_e[ya, zs]]), "col", axis=2, tiled=True
    )
    coup_full = gathered[1]
    half_ey_full = solve_local(gathered[0], coup_full, 1)
    pos_y = (
        lax.axis_index("row") * count_y
        + lax.broadcasted_iota(jnp.int32, (count_y + 1, 1, 1), 0)
        - 1
    )
    half_ey_full = jnp.where(pos_y >= 0, half_ey_full, 0.0)
    padded = jnp.pad(half_ey_full, ((0, 0), (1, 1), (0, 0)))
    half_ey_e = lax.dynamic_slice_in_dim(padded, col_index * count_z, count_z + 2, axis=1)

    half_ez_e = solve_local(source_z, coup_e[ys, za], 2)
    half_ez_e = jnp.where(inside[ys, za], half_ez_e, 0.0)

    half_hy_e = hy_e[ys, za] + HALF_STEP * (diff_up(half_ez_e, 2) - dpz_ex)
    half_hy_e = jnp.where(inside[ys, za], half_hy_e, 0.0)
    dz_half_ey = half_ey_e[:, 1:] - half_ey_e[:, :-1]
    half_hx_e = hx_e[ya, za] + HALF_STEP * (dz_half_ey[:, 0 : count_z + 1] - dpy_ez)
    half_hx_e = jnp.where(inside[ya, za], half_hx_e, 0.0)

    half_ey = half_ey_e[1 : count_y + 1, 1 : count_z + 1]
    half_ez = half_ez_e[:, 1:]
    dx_half_ez = diff_up(half_ez_e, 2)
    dz_ey_own = dz_half_ey[:, 1 : count_z + 1]
    second_z = keep * half_ez + drive * (
        diff_down(half_hy_e[:, 1:], 2)
        - (half_hx_e[1:, 1:] - half_hx_e[:-1, 1:])
        - HALF_STEP * (dz_ey_own[1:] - dz_ey_own[:-1])
    )

    system = RowSystem(coupling)
    bwd_x, head_x, tail_x = system.reduce_source(source_x)
    bwd_z, head_z, tail_z = system.reduce_source(second_z)
    parts = rows
    payload = jnp.stack(
        [
            jnp.stack(system.head + [head_x, head_z]),
            jnp.stack(system.tail + [tail_x, tail_z]),
        ],
        1,
    )
    payload = to_solver(payload, parts)
    received = lax.all_to_all(payload, "row", split_axis=0, concat_axis=0, tiled=True)
    width = received.shape[-1]
    received = jnp.transpose(received, (1, 0, 2, 3)).reshape((5, parts * 2, width))
    answer = reduced_solve(received[:3], received[3:], True)
    back = lax.all_to_all(answer, "row", split_axis=0, concat_axis=0, tiled=True)
    bounds = from_solver(back, count_z, count_x)
    half_ex_rows = system.expand(bwd_x, bounds[0], bounds[1])
    half_ex_e = jnp.stack([bounds[6]] + half_ex_rows + [bounds[4]])
    next_ez_rows = system.expand(bwd_z, bounds[2], bounds[3])
    next_ez = jnp.stack(next_ez_rows)
    next_ez_e = jnp.stack(next_ez_rows + [bounds[5]])

    half_hz_e = hz_e[ya, zs] + HALF_STEP * (
        (half_ex_e[1:] - half_ex_e[:-1]) - diff_up(ey_e[ya, zs], 2)
    )
    half_hz_e = jnp.where(inside[ya, zs], half_hz_e, 0.0)

    half_ex = half_ex_e[1 : count_y + 1]
    dy_half_ex = half_ex_e[2:] - half_ex_e[1:-1]
    second_x = keep * half_ex + drive * (
        (half_hz_e[1:] - half_hz_e[:-1])
        - (half_hy_e[:, 1:] - half_hy_e[:, :-1])
        - HALF_STEP * (dx_half_ez[:, 1:] - dx_half_ez[:, :-1])
    )
    second_y = keep * half_ey + drive * (
        (half_hx_e[1:, 1:] - half_hx_e[1:, :-1])
        - diff_down(half_hz_e[1:], 2)
        - HALF_STEP * diff_down(dy_half_ex, 2)
    )

    second_full = lax.all_gather(second_x, "col", axis=1, tiled=True)
    next_ex_full = solve_local(second_full, coup_full[1:], 1)
    padded = jnp.pad(next_ex_full, ((0, 0), (0, 1), (0, 0)))
    next_ex_e = lax.dynamic_slice_in_dim(padded, col_index * count_z, count_z + 1, axis=1)
    next_ex = next_ex_e[:, :-1]

    next_ey = solve_local(second_y, coupling, 2)

    next_hx = half_hx_e[1:, 1:] + HALF_STEP * (
        dz_ey_own[1:] - (next_ez_e[1:] - next_ez_e[:-1])
    )
    next_hy = half_hy_e[:, 1:] + HALF_STEP * (
        dx_half_ez[:, 1:] - (next_ex_e[:, 1:] - next_ex_e[:, :-1])
    )
    next_hz = half_hz_e[1:] + HALF_STEP * (dy_half_ex - diff_up(next_ey, 2))
    return (next_ex, next_ey, next_ez, next_hx, next_hy, next_hz)


def solution(mesh):
    spec = P("row", "col", None)
    return jax.shard_map(
        on_device,
        mesh=mesh,
        in_specs=(spec,) * 8,
        out_specs=(spec,) * 6,
        check_vma=False,
    )
```

```python
import jax
import jax.numpy as jnp
from jax import lax
from jax.sharding import PartitionSpec as P

HALF_STEP = 30.0


def with_halo(cells, sides, width):
    for axis, dim in sides:
        count = lax.axis_size(axis)
        ends = count - 1
        head = lax.slice_in_dim(cells, 0, width, axis=dim)
        tail = lax.slice_in_dim(cells, cells.shape[dim] - width, cells.shape[dim], axis=dim)
        cells = jnp.concatenate(
            [
                lax.ppermute(tail, axis, [(i, (i + 1) % count) for i in range(ends)]),
                cells,
                lax.ppermute(head, axis, [((i + 1) % count, i) for i in range(ends)]),
            ],
            axis=dim,
        )
    return cells


def shifted(values, stride, line_axis, filler, forward):
    length = values.shape[line_axis]
    padding = jnp.full_like(lax.slice_in_dim(values, 0, stride, axis=line_axis), filler)
    if forward:
        return jnp.concatenate(
            [lax.slice_in_dim(values, stride, length, axis=line_axis), padding], line_axis
        )
    return jnp.concatenate(
        [padding, lax.slice_in_dim(values, 0, length - stride, axis=line_axis)], line_axis
    )


def diff_up(values, line_axis):
    return shifted(values, 1, line_axis, 0.0, True) - values


def diff_down(values, line_axis):
    return values - shifted(values, 1, line_axis, 0.0, False)


def reduce_lines(sub_diag, main_diag, super_diag, source, line_axis):
    length = source.shape[line_axis]
    stride = 1
    while stride < length:
        sub_lo = shifted(sub_diag, stride, line_axis, 0.0, False)
        mid_lo = shifted(main_diag, stride, line_axis, 1.0, False)
        sup_lo = shifted(super_diag, stride, line_axis, 0.0, False)
        src_lo = shifted(source, stride, line_axis, 0.0, False)
        sub_hi = shifted(sub_diag, stride, line_axis, 0.0, True)
        mid_hi = shifted(main_diag, stride, line_axis, 1.0, True)
        sup_hi = shifted(super_diag, stride, line_axis, 0.0, True)
        src_hi = shifted(source, stride, line_axis, 0.0, True)
        ratio_lo = sub_diag / mid_lo
        ratio_hi = super_diag / mid_hi
        sub_diag = -sub_lo * ratio_lo
        super_diag = -sup_hi * ratio_hi
        main_diag = main_diag - sup_lo * ratio_lo - sub_hi * ratio_hi
        source = source - src_lo * ratio_lo - src_hi * ratio_hi
        stride = stride * 2
    return source / main_diag


def line_flags(length, line_axis, rank):
    iota_shape = [1] * rank
    iota_shape[line_axis] = length
    where_line = lax.broadcasted_iota(jnp.int32, tuple(iota_shape), line_axis)
    return (where_line == 0, where_line == length - 1)


def line_system(coupling, is_first, is_final):
    sub_diag = jnp.where(is_first, 0.0, -coupling)
    main_diag = jnp.where(is_first, 1.0 + coupling, 1.0 + 2.0 * coupling)
    super_diag = jnp.where(is_final, 0.0, -coupling)
    return (sub_diag, main_diag, super_diag)


def solve_local(source, coupling, line_axis):
    is_first, is_final = line_flags(source.shape[line_axis], line_axis, source.ndim)
    sub_diag, main_diag, super_diag = line_system(coupling, is_first, is_final)
    return reduce_lines(sub_diag, main_diag, super_diag, source, line_axis)


def inside_mask(count_y, count_z):
    pos_y = (
        lax.axis_index("row") * count_y
        + lax.broadcasted_iota(jnp.int32, (count_y + 2, 1, 1), 0)
        - 1
    )
    pos_z = (
        lax.axis_index("col") * count_z
        + lax.broadcasted_iota(jnp.int32, (1, count_z + 2, 1), 1)
        - 1
    )
    inside = (
        (pos_y >= 0)
        & (pos_y < count_y * lax.axis_size("row"))
        & (pos_z >= 0)
        & (pos_z < count_z * lax.axis_size("col"))
    )
    return inside


class RowSystem:
    def __init__(self, coupling):
        count = coupling.shape[0]
        self.count = count
        row_index = lax.axis_index("row")
        is_first, is_final = line_flags(count, 0, 3)
        is_first = jnp.logical_and(is_first, row_index == 0)
        is_final = jnp.logical_and(is_final, row_index == lax.axis_size("row") - 1)
        sub, main, sup = line_system(coupling, is_first, is_final)
        self.sub, self.main, self.sup = sub, main, sup
        fwd_sub = [None] * count
        fwd_sup = [None] * count
        pivot = [None] * count
        pivot[1] = main[1]
        fwd_sub[1] = sub[1] / main[1]
        fwd_sup[1] = sup[1] / main[1]
        for level in range(2, count - 1):
            pivot[level] = main[level] - sub[level] * fwd_sup[level - 1]
            fwd_sub[level] = -sub[level] * fwd_sub[level - 1] / pivot[level]
            fwd_sup[level] = sup[level] / pivot[level]
        bwd_sub = [None] * count
        bwd_sup = [None] * count
        bwd_sub[count - 2] = fwd_sub[count - 2]
        bwd_sup[count - 2] = fwd_sup[count - 2]
        for level in range(count - 3, 0, -1):
            bwd_sub[level] = fwd_sub[level] - fwd_sup[level] * bwd_sub[level + 1]
            bwd_sup[level] = -fwd_sup[level] * bwd_sup[level + 1]
        last = count - 1
        self.pivot, self.fwd_sub, self.fwd_sup = pivot, fwd_sub, fwd_sup
        self.bwd_sub, self.bwd_sup = bwd_sub, bwd_sup
        self.head = [sub[0], main[0] - sup[0] * bwd_sub[1], -sup[0] * bwd_sup[1]]
        self.tail = [
            -sub[last] * fwd_sub[last - 1],
            main[last] - sub[last] * fwd_sup[last - 1],
            sup[last],
        ]

    def reduce_source(self, source):
        count = self.count
        sub = self.sub
        fwd_src = [None] * count
        fwd_src[1] = source[1] / self.pivot[1]
        for level in range(2, count - 1):
            fwd_src[level] = (source[level] - sub[level] * fwd_src[level - 1]) / self.pivot[level]
        bwd_src = [None] * count
        bwd_src[count - 2] = fwd_src[count - 2]
        for level in range(count - 3, 0, -1):
            bwd_src[level] = fwd_src[level] - self.fwd_sup[level] * bwd_src[level + 1]
        last = count - 1
        head_src = source[0] - self.sup[0] * bwd_src[1]
        tail_src = source[last] - sub[last] * fwd_src[last - 1]
        return bwd_src, head_src, tail_src

    def expand(self, bwd_src, first_vals, final_vals):
        rows = [first_vals]
        for level in range(1, self.count - 1):
            rows.append(
                bwd_src[level] - self.bwd_sub[level] * first_vals - self.bwd_sup[level] * final_vals
            )
        rows.append(final_vals)
        return rows


def to_solver(planes, parts):
    lead = planes.shape[:-2]
    count_z, count_x = planes.shape[-2:]
    per_z = parts // count_z
    width = count_x // per_z
    split = planes.reshape(lead + (count_z, per_z, width))
    rank = len(lead)
    order = (rank, rank + 1) + tuple(range(rank)) + (rank + 2,)
    split = jnp.transpose(split, order)
    return split.reshape((parts,) + lead + (width,))


def from_solver(chunks, count_z, count_x):
    parts, k, width = chunks.shape
    per_z = parts // count_z
    split = chunks.reshape((count_z, per_z, k, width))
    split = jnp.transpose(split, (2, 0, 1, 3))
    return split.reshape((k, count_z, count_x))


def reduced_solve(matrix, rhs, want_prev):
    solved = reduce_lines(matrix[0][None], matrix[1][None], matrix[2][None], rhs, 1)
    parts = solved.shape[1] // 2
    outs = []
    for one in range(solved.shape[0]):
        pairs = solved[one].reshape((parts, 2) + solved.shape[2:])
        heads = pairs[:, 0]
        tails = pairs[:, 1]
        zero = jnp.zeros_like(heads[:1])
        outs += [heads, tails]
    for one in range(solved.shape[0]):
        heads = outs[2 * one]
        outs.append(jnp.concatenate([heads[1:], zero], 0))
    outs.append(jnp.concatenate([zero, outs[1][:-1]], 0))
    return jnp.stack(outs, 1)


def shift_rows(values, distance, filler):
    rows = lax.axis_size("row")
    step = abs(distance)
    if distance > 0:
        pairs = [(i, i + step) for i in range(rows - step)]
    else:
        pairs = [(i + step, i) for i in range(rows - step)]
    moved = lax.ppermute(values, "row", pairs)
    if filler is None:
        return moved
    row_index = lax.axis_index("row")
    valid = (row_index - distance >= 0) & (row_index - distance < rows)
    return jnp.where(valid, moved, filler)


def distributed_reduce(sub, main, sup, src):
    rows = lax.axis_size("row")
    nrhs = src.shape[0]
    stride = 1
    while stride < 2 * rows:
        if stride == 1:
            to_next = jnp.concatenate([jnp.stack([sub[1], main[1], sup[1]]), src[:, 1]], 0)
            to_prev = jnp.concatenate([jnp.stack([sub[0], main[0], sup[0]]), src[:, 0]], 0)
            got_prev = shift_rows(to_next, 1, None)
            got_next = shift_rows(to_prev, -1, None)
            valid_prev = lax.axis_index("row") >= 1
            valid_next = lax.axis_index("row") < rows - 1
            sub_lo = jnp.stack([got_prev[0], sub[0]])
            mid_lo = jnp.stack([jnp.where(valid_prev, got_prev[1], 1.0), main[0]])
            sup_lo = jnp.stack([got_prev[2], sup[0]])
            src_lo = jnp.stack([got_prev[3:], src[:, 0]], 1)
            sub_hi = jnp.stack([sub[1], got_next[0]])
            mid_hi = jnp.stack([main[1], jnp.where(valid_next, got_next[1], 1.0)])
            sup_hi = jnp.stack([sup[1], got_next[2]])
            src_hi = jnp.stack([src[:, 1], got_next[3:]], 1)
        else:
            dist = stride // 2
            packed = jnp.concatenate([jnp.stack([sub, main, sup]), src], 0)
            got_prev = shift_rows(packed, dist, None)
            got_next = shift_rows(packed, -dist, None)
            row_index = lax.axis_index("row")
            sub_lo, sup_lo, src_lo = got_prev[0], got_prev[2], got_prev[3:]
            mid_lo = jnp.where(row_index >= dist, got_prev[1], 1.0)
            sub_hi, sup_hi, src_hi = got_next[0], got_next[2], got_next[3:]
            mid_hi = jnp.where(row_index < rows - dist, got_next[1], 1.0)
        ratio_lo = sub / mid_lo
        ratio_hi = sup / mid_hi
        sub = -sub_lo * ratio_lo
        sup = -sup_hi * ratio_hi
        main = main - sup_lo * ratio_lo - sub_hi * ratio_hi
        src = src - src_lo * ratio_lo - src_hi * ratio_hi
        stride = stride * 2
    return src / main


def field_halos(fields):
    rows = lax.axis_size("row")
    cols = lax.axis_size("col")
    down_rows = [(i, i + 1) for i in range(rows - 1)]
    up_rows = [(i + 1, i) for i in range(rows - 1)]
    down_cols = [(i, i + 1) for i in range(cols - 1)]
    up_cols = [(i + 1, i) for i in range(cols - 1)]
    from_prev = lax.ppermute(jnp.stack([f[-1:] for f in fields]), "row", down_rows)
    from_next = lax.ppermute(jnp.stack([f[:1] for f in fields]), "row", up_rows)
    ext_y = [
        jnp.concatenate([from_prev[k], f, from_next[k]], 0) for k, f in enumerate(fields)
    ]
    from_left = lax.ppermute(jnp.stack([e[:, -1:] for e in ext_y]), "col", down_cols)
    from_right = lax.ppermute(jnp.stack([e[:, :1] for e in ext_y]), "col", up_cols)
    return [
        jnp.concatenate([from_left[k], e, from_right[k]], 1) for k, e in enumerate(ext_y)
    ]


def on_device(
    efield_x, efield_y, efield_z, hfield_x, hfield_y, hfield_z, permittivity, conductivity
):
    count_y = efield_x.shape[0]
    count_z = efield_x.shape[1]
    count_x = efield_x.shape[2]
    rows = lax.axis_size("row")
    col_index = lax.axis_index("col")

    ext = field_halos(
        [efield_x, efield_y, efield_z, hfield_x, hfield_y, hfield_z, permittivity, conductivity]
    )
    inside = inside_mask(count_y, count_z)
    ex_e, ey_e, ez_e = ext[0], ext[1], ext[2]
    hx_e, hy_e, hz_e = ext[3], ext[4], ext[5]
    eps_e = jnp.where(inside, ext[6], 1.0)
    sig_e = jnp.where(inside, ext[7], 0.0)
    damping = sig_e * HALF_STEP / (2.0 * eps_e)
    keep_e = (1.0 - damping) / (1.0 + damping)
    drive_e = HALF_STEP / (eps_e * (1.0 + damping))
    coup_e = drive_e * HALF_STEP

    ys = slice(1, count_y + 1)
    zs = slice(1, count_z + 1)
    keep = keep_e[ys, zs]
    drive = drive_e[ys, zs]
    coupling = coup_e[ys, zs]

    dpx_ey = diff_up(ey_e[0 : count_y + 1, zs], 2)
    source_x = keep * efield_x + drive * (
        (hz_e[ys, zs] - hz_e[0:count_y, zs])
        - (hy_e[ys, zs] - hy_e[ys, 0:count_z])
        - HALF_STEP * (dpx_ey[1:] - dpx_ey[:-1])
    )
    ya = slice(0, count_y + 1)
    dpy_ez = ez_e[1 : count_y + 2, 0 : count_z + 1] - ez_e[0 : count_y + 1, 0 : count_z + 1]
    source_y = keep_e[ya, zs] * ey_e[ya, zs] + drive_e[ya, zs] * (
        (hx_e[ya, zs] - hx_e[ya, 0:count_z])
        - diff_down(hz_e[ya, zs], 2)
        - HALF_STEP * (dpy_ez[:, 1:] - dpy_ez[:, :-1])
    )
    za = slice(0, count_z + 1)
    dpz_ex = ex_e[ys, 1 : count_z + 2] - ex_e[ys, 0 : count_z + 1]
    source_z = keep_e[ys, za] * ez_e[ys, za] + drive_e[ys, za] * (
        diff_down(hy_e[ys, za], 2)
        - (hx_e[ys, za] - hx_e[0:count_y, za])
        - HALF_STEP * diff_down(dpz_ex, 2)
    )

    gathered = lax.all_gather(
        jnp.stack([source_y, coup_e[ya, zs]]), "col", axis=2, tiled=True
    )
    coup_full = gathered[1]
    half_ey_full = solve_local(gathered[0], coup_full, 1)
    pos_y = (
        lax.axis_index("row") * count_y
        + lax.broadcasted_iota(jnp.int32, (count_y + 1, 1, 1), 0)
        - 1
    )
    half_ey_full = jnp.where(pos_y >= 0, half_ey_full, 0.0)
    padded = jnp.pad(half_ey_full, ((0, 0), (1, 1), (0, 0)))
    half_ey_e = lax.dynamic_slice_in_dim(padded, col_index * count_z, count_z + 2, axis=1)

    half_ez_e = solve_local(source_z, coup_e[ys, za], 2)
    half_ez_e = jnp.where(inside[ys, za], half_ez_e, 0.0)

    half_hy_e = hy_e[ys, za] + HALF_STEP * (diff_up(half_ez_e, 2) - dpz_ex)
    half_hy_e = jnp.where(inside[ys, za], half_hy_e, 0.0)
    dz_half_ey = half_ey_e[:, 1:] - half_ey_e[:, :-1]
    half_hx_e = hx_e[ya, za] + HALF_STEP * (dz_half_ey[:, 0 : count_z + 1] - dpy_ez)
    half_hx_e = jnp.where(inside[ya, za], half_hx_e, 0.0)

    half_ey = half_ey_e[1 : count_y + 1, 1 : count_z + 1]
    half_ez = half_ez_e[:, 1:]
    dx_half_ez = diff_up(half_ez_e, 2)
    dz_ey_own = dz_half_ey[:, 1 : count_z + 1]
    second_z = keep * half_ez + drive * (
        diff_down(half_hy_e[:, 1:], 2)
        - (half_hx_e[1:, 1:] - half_hx_e[:-1, 1:])
        - HALF_STEP * (dz_ey_own[1:] - dz_ey_own[:-1])
    )

    system = RowSystem(coupling)
    bwd_x, head_x, tail_x = system.reduce_source(source_x)
    bwd_z, head_z, tail_z = system.reduce_source(second_z)
    solved = distributed_reduce(
        jnp.stack([system.head[0], system.tail[0]]),
        jnp.stack([system.head[1], system.tail[1]]),
        jnp.stack([system.head[2], system.tail[2]]),
        jnp.stack([jnp.stack([head_x, tail_x]), jnp.stack([head_z, tail_z])]),
    )
    prev_tail = shift_rows(solved[0, 1], 1, None)
    next_heads = shift_rows(solved[:, 0], -1, None)
    bounds = [
        solved[0, 0], solved[0, 1], solved[1, 0], solved[1, 1],
        next_heads[0], next_heads[1], prev_tail,
    ]
    half_ex_rows = system.expand(bwd_x, bounds[0], bounds[1])
    half_ex_e = jnp.stack([bounds[6]] + half_ex_rows + [bounds[4]])
    next_ez_rows = system.expand(bwd_z, bounds[2], bounds[3])
    next_ez = jnp.stack(next_ez_rows)
    next_ez_e = jnp.stack(next_ez_rows + [bounds[5]])

    half_hz_e = hz_e[ya, zs] + HALF_STEP * (
        (half_ex_e[1:] - half_ex_e[:-1]) - diff_up(ey_e[ya, zs], 2)
    )
    half_hz_e = jnp.where(inside[ya, zs], half_hz_e, 0.0)

    half_ex = half_ex_e[1 : count_y + 1]
    dy_half_ex = half_ex_e[2:] - half_ex_e[1:-1]
    second_x = keep * half_ex + drive * (
        (half_hz_e[1:] - half_hz_e[:-1])
        - (half_hy_e[:, 1:] - half_hy_e[:, :-1])
        - HALF_STEP * (dx_half_ez[:, 1:] - dx_half_ez[:, :-1])
    )
    second_y = keep * half_ey + drive * (
        (half_hx_e[1:, 1:] - half_hx_e[1:, :-1])
        - diff_down(half_hz_e[1:], 2)
        - HALF_STEP * diff_down(dy_half_ex, 2)
    )

    second_full = lax.all_gather(second_x, "col", axis=1, tiled=True)
    next_ex_full = solve_local(second_full, coup_full[1:], 1)
    padded = jnp.pad(next_ex_full, ((0, 0), (0, 1), (0, 0)))
    next_ex_e = lax.dynamic_slice_in_dim(padded, col_index * count_z, count_z + 1, axis=1)
    next_ex = next_ex_e[:, :-1]

    next_ey = solve_local(second_y, coupling, 2)

    next_hx = half_hx_e[1:, 1:] + HALF_STEP * (
        dz_ey_own[1:] - (next_ez_e[1:] - next_ez_e[:-1])
    )
    next_hy = half_hy_e[:, 1:] + HALF_STEP * (
        dx_half_ez[:, 1:] - (next_ex_e[:, 1:] - next_ex_e[:, :-1])
    )
    next_hz = half_hz_e[1:] + HALF_STEP * (dy_half_ex - diff_up(next_ey, 2))
    return (next_ex, next_ey, next_ez, next_hx, next_hy, next_hz)


def solution(mesh):
    spec = P("row", "col", None)
    return jax.shard_map(
        on_device,
        mesh=mesh,
        in_specs=(spec,) * 8,
        out_specs=(spec,) * 6,
        check_vma=False,
    )
```

```python
import jax
import jax.numpy as jnp
from jax import lax
from jax.sharding import PartitionSpec as P

HALF_STEP = 30.0


def with_halo(cells, sides, width):
    for axis, dim in sides:
        count = lax.axis_size(axis)
        ends = count - 1
        head = lax.slice_in_dim(cells, 0, width, axis=dim)
        tail = lax.slice_in_dim(cells, cells.shape[dim] - width, cells.shape[dim], axis=dim)
        cells = jnp.concatenate(
            [
                lax.ppermute(tail, axis, [(i, (i + 1) % count) for i in range(ends)]),
                cells,
                lax.ppermute(head, axis, [((i + 1) % count, i) for i in range(ends)]),
            ],
            axis=dim,
        )
    return cells


def shifted(values, stride, line_axis, filler, forward):
    length = values.shape[line_axis]
    padding = jnp.full_like(lax.slice_in_dim(values, 0, stride, axis=line_axis), filler)
    if forward:
        return jnp.concatenate(
            [lax.slice_in_dim(values, stride, length, axis=line_axis), padding], line_axis
        )
    return jnp.concatenate(
        [padding, lax.slice_in_dim(values, 0, length - stride, axis=line_axis)], line_axis
    )


def diff_up(values, line_axis):
    return shifted(values, 1, line_axis, 0.0, True) - values


def diff_down(values, line_axis):
    return values - shifted(values, 1, line_axis, 0.0, False)


def reduce_lines(sub_diag, main_diag, super_diag, source, line_axis):
    length = source.shape[line_axis]
    stride = 1
    while stride < length:
        sub_lo = shifted(sub_diag, stride, line_axis, 0.0, False)
        mid_lo = shifted(main_diag, stride, line_axis, 1.0, False)
        sup_lo = shifted(super_diag, stride, line_axis, 0.0, False)
        src_lo = shifted(source, stride, line_axis, 0.0, False)
        sub_hi = shifted(sub_diag, stride, line_axis, 0.0, True)
        mid_hi = shifted(main_diag, stride, line_axis, 1.0, True)
        sup_hi = shifted(super_diag, stride, line_axis, 0.0, True)
        src_hi = shifted(source, stride, line_axis, 0.0, True)
        ratio_lo = sub_diag / mid_lo
        ratio_hi = super_diag / mid_hi
        sub_diag = -sub_lo * ratio_lo
        super_diag = -sup_hi * ratio_hi
        main_diag = main_diag - sup_lo * ratio_lo - sub_hi * ratio_hi
        source = source - src_lo * ratio_lo - src_hi * ratio_hi
        stride = stride * 2
    return source / main_diag


def line_flags(length, line_axis, rank):
    iota_shape = [1] * rank
    iota_shape[line_axis] = length
    where_line = lax.broadcasted_iota(jnp.int32, tuple(iota_shape), line_axis)
    return (where_line == 0, where_line == length - 1)


def line_system(coupling, is_first, is_final):
    sub_diag = jnp.where(is_first, 0.0, -coupling)
    main_diag = jnp.where(is_first, 1.0 + coupling, 1.0 + 2.0 * coupling)
    super_diag = jnp.where(is_final, 0.0, -coupling)
    return (sub_diag, main_diag, super_diag)


def solve_local(source, coupling, line_axis):
    is_first, is_final = line_flags(source.shape[line_axis], line_axis, source.ndim)
    sub_diag, main_diag, super_diag = line_system(coupling, is_first, is_final)
    return reduce_lines(sub_diag, main_diag, super_diag, source, line_axis)


def inside_mask(count_y, count_z):
    pos_y = (
        lax.axis_index("row") * count_y
        + lax.broadcasted_iota(jnp.int32, (count_y + 2, 1, 1), 0)
        - 1
    )
    pos_z = (
        lax.axis_index("col") * count_z
        + lax.broadcasted_iota(jnp.int32, (1, count_z + 2, 1), 1)
        - 1
    )
    inside = (
        (pos_y >= 0)
        & (pos_y < count_y * lax.axis_size("row"))
        & (pos_z >= 0)
        & (pos_z < count_z * lax.axis_size("col"))
    )
    return inside


class RowSystem:
    def __init__(self, coupling):
        count = coupling.shape[0]
        self.count = count
        row_index = lax.axis_index("row")
        is_first, is_final = line_flags(count, 0, 3)
        is_first = jnp.logical_and(is_first, row_index == 0)
        is_final = jnp.logical_and(is_final, row_index == lax.axis_size("row") - 1)
        sub, main, sup = line_system(coupling, is_first, is_final)
        self.sub, self.main, self.sup = sub, main, sup
        fwd_sub = [None] * count
        fwd_sup = [None] * count
        pivot = [None] * count
        pivot[1] = main[1]
        fwd_sub[1] = sub[1] / main[1]
        fwd_sup[1] = sup[1] / main[1]
        for level in range(2, count - 1):
            pivot[level] = main[level] - sub[level] * fwd_sup[level - 1]
            fwd_sub[level] = -sub[level] * fwd_sub[level - 1] / pivot[level]
            fwd_sup[level] = sup[level] / pivot[level]
        bwd_sub = [None] * count
        bwd_sup = [None] * count
        bwd_sub[count - 2] = fwd_sub[count - 2]
        bwd_sup[count - 2] = fwd_sup[count - 2]
        for level in range(count - 3, 0, -1):
            bwd_sub[level] = fwd_sub[level] - fwd_sup[level] * bwd_sub[level + 1]
            bwd_sup[level] = -fwd_sup[level] * bwd_sup[level + 1]
        last = count - 1
        self.pivot, self.fwd_sub, self.fwd_sup = pivot, fwd_sub, fwd_sup
        self.bwd_sub, self.bwd_sup = bwd_sub, bwd_sup
        self.head = [sub[0], main[0] - sup[0] * bwd_sub[1], -sup[0] * bwd_sup[1]]
        self.tail = [
            -sub[last] * fwd_sub[last - 1],
            main[last] - sub[last] * fwd_sup[last - 1],
            sup[last],
        ]

    def reduce_source(self, source):
        count = self.count
        sub = self.sub
        fwd_src = [None] * count
        fwd_src[1] = source[1] / self.pivot[1]
        for level in range(2, count - 1):
            fwd_src[level] = (source[level] - sub[level] * fwd_src[level - 1]) / self.pivot[level]
        bwd_src = [None] * count
        bwd_src[count - 2] = fwd_src[count - 2]
        for level in range(count - 3, 0, -1):
            bwd_src[level] = fwd_src[level] - self.fwd_sup[level] * bwd_src[level + 1]
        last = count - 1
        head_src = source[0] - self.sup[0] * bwd_src[1]
        tail_src = source[last] - sub[last] * fwd_src[last - 1]
        return bwd_src, head_src, tail_src

    def expand(self, bwd_src, first_vals, final_vals):
        rows = [first_vals]
        for level in range(1, self.count - 1):
            rows.append(
                bwd_src[level] - self.bwd_sub[level] * first_vals - self.bwd_sup[level] * final_vals
            )
        rows.append(final_vals)
        return rows


def to_solver(planes, parts):
    lead = planes.shape[:-2]
    count_z, count_x = planes.shape[-2:]
    per_z = parts // count_z
    width = count_x // per_z
    split = planes.reshape(lead + (count_z, per_z, width))
    rank = len(lead)
    order = (rank, rank + 1) + tuple(range(rank)) + (rank + 2,)
    split = jnp.transpose(split, order)
    return split.reshape((parts,) + lead + (width,))


def from_solver(chunks, count_z, count_x):
    parts, k, width = chunks.shape
    per_z = parts // count_z
    split = chunks.reshape((count_z, per_z, k, width))
    split = jnp.transpose(split, (2, 0, 1, 3))
    return split.reshape((k, count_z, count_x))


def reduced_solve(matrix, rhs, want_prev):
    solved = reduce_lines(matrix[0][None], matrix[1][None], matrix[2][None], rhs, 1)
    parts = solved.shape[1] // 2
    outs = []
    for one in range(solved.shape[0]):
        pairs = solved[one].reshape((parts, 2) + solved.shape[2:])
        heads = pairs[:, 0]
        tails = pairs[:, 1]
        zero = jnp.zeros_like(heads[:1])
        outs += [heads, tails]
    for one in range(solved.shape[0]):
        heads = outs[2 * one]
        outs.append(jnp.concatenate([heads[1:], zero], 0))
    outs.append(jnp.concatenate([zero, outs[1][:-1]], 0))
    return jnp.stack(outs, 1)


def gather_cols(block, axis):
    cols = lax.axis_size("col")
    col_index = lax.axis_index("col")
    got = [block]
    for shift in range(1, cols):
        got.append(lax.ppermute(block, "col", [(i, (i + shift) % cols) for i in range(cols)]))
    pieces = []
    for place in range(cols):
        shift_needed = (col_index - place) % cols
        piece = got[0]
        for shift in range(1, cols):
            piece = jnp.where(shift_needed == shift, got[shift], piece)
        pieces.append(piece)
    return jnp.concatenate(pieces, axis)


def field_halos(fields):
    rows = lax.axis_size("row")
    cols = lax.axis_size("col")
    down_rows = [(i, i + 1) for i in range(rows - 1)]
    up_rows = [(i + 1, i) for i in range(rows - 1)]
    down_cols = [(i, i + 1) for i in range(cols - 1)]
    up_cols = [(i + 1, i) for i in range(cols - 1)]
    from_prev = lax.ppermute(jnp.stack([f[-1:] for f in fields]), "row", down_rows)
    from_next = lax.ppermute(jnp.stack([f[:1] for f in fields]), "row", up_rows)
    ext_y = [
        jnp.concatenate([from_prev[k], f, from_next[k]], 0) for k, f in enumerate(fields)
    ]
    from_left = lax.ppermute(jnp.stack([e[:, -1:] for e in ext_y]), "col", down_cols)
    from_right = lax.ppermute(jnp.stack([e[:, :1] for e in ext_y]), "col", up_cols)
    return [
        jnp.concatenate([from_left[k], e, from_right[k]], 1) for k, e in enumerate(ext_y)
    ]


def on_device(
    efield_x, efield_y, efield_z, hfield_x, hfield_y, hfield_z, permittivity, conductivity
):
    count_y = efield_x.shape[0]
    count_z = efield_x.shape[1]
    count_x = efield_x.shape[2]
    rows = lax.axis_size("row")
    col_index = lax.axis_index("col")

    ext = field_halos(
        [efield_x, efield_y, efield_z, hfield_x, hfield_y, hfield_z, permittivity, conductivity]
    )
    inside = inside_mask(count_y, count_z)
    ex_e, ey_e, ez_e = ext[0], ext[1], ext[2]
    hx_e, hy_e, hz_e = ext[3], ext[4], ext[5]
    eps_e = jnp.where(inside, ext[6], 1.0)
    sig_e = jnp.where(inside, ext[7], 0.0)
    damping = sig_e * HALF_STEP / (2.0 * eps_e)
    keep_e = (1.0 - damping) / (1.0 + damping)
    drive_e = HALF_STEP / (eps_e * (1.0 + damping))
    coup_e = drive_e * HALF_STEP

    ys = slice(1, count_y + 1)
    zs = slice(1, count_z + 1)
    keep = keep_e[ys, zs]
    drive = drive_e[ys, zs]
    coupling = coup_e[ys, zs]

    dpx_ey = diff_up(ey_e[0 : count_y + 1, zs], 2)
    source_x = keep * efield_x + drive * (
        (hz_e[ys, zs] - hz_e[0:count_y, zs])
        - (hy_e[ys, zs] - hy_e[ys, 0:count_z])
        - HALF_STEP * (dpx_ey[1:] - dpx_ey[:-1])
    )
    ya = slice(0, count_y + 1)
    dpy_ez = ez_e[1 : count_y + 2, 0 : count_z + 1] - ez_e[0 : count_y + 1, 0 : count_z + 1]
    source_y = keep_e[ya, zs] * ey_e[ya, zs] + drive_e[ya, zs] * (
        (hx_e[ya, zs] - hx_e[ya, 0:count_z])
        - diff_down(hz_e[ya, zs], 2)
        - HALF_STEP * (dpy_ez[:, 1:] - dpy_ez[:, :-1])
    )
    za = slice(0, count_z + 1)
    dpz_ex = ex_e[ys, 1 : count_z + 2] - ex_e[ys, 0 : count_z + 1]
    source_z = keep_e[ys, za] * ez_e[ys, za] + drive_e[ys, za] * (
        diff_down(hy_e[ys, za], 2)
        - (hx_e[ys, za] - hx_e[0:count_y, za])
        - HALF_STEP * diff_down(dpz_ex, 2)
    )

    gathered = gather_cols(jnp.stack([source_y, coup_e[ya, zs]]), 2)
    coup_full = gathered[1]
    half_ey_full = solve_local(gathered[0], coup_full, 1)
    pos_y = (
        lax.axis_index("row") * count_y
        + lax.broadcasted_iota(jnp.int32, (count_y + 1, 1, 1), 0)
        - 1
    )
    half_ey_full = jnp.where(pos_y >= 0, half_ey_full, 0.0)
    padded = jnp.pad(half_ey_full, ((0, 0), (1, 1), (0, 0)))
    half_ey_e = lax.dynamic_slice_in_dim(padded, col_index * count_z, count_z + 2, axis=1)

    half_ez_e = solve_local(source_z, coup_e[ys, za], 2)
    half_ez_e = jnp.where(inside[ys, za], half_ez_e, 0.0)

    half_hy_e = hy_e[ys, za] + HALF_STEP * (diff_up(half_ez_e, 2) - dpz_ex)
    half_hy_e = jnp.where(inside[ys, za], half_hy_e, 0.0)
    dz_half_ey = half_ey_e[:, 1:] - half_ey_e[:, :-1]
    half_hx_e = hx_e[ya, za] + HALF_STEP * (dz_half_ey[:, 0 : count_z + 1] - dpy_ez)
    half_hx_e = jnp.where(inside[ya, za], half_hx_e, 0.0)

    half_ey = half_ey_e[1 : count_y + 1, 1 : count_z + 1]
    half_ez = half_ez_e[:, 1:]
    dx_half_ez = diff_up(half_ez_e, 2)
    dz_ey_own = dz_half_ey[:, 1 : count_z + 1]
    second_z = keep * half_ez + drive * (
        diff_down(half_hy_e[:, 1:], 2)
        - (half_hx_e[1:, 1:] - half_hx_e[:-1, 1:])
        - HALF_STEP * (dz_ey_own[1:] - dz_ey_own[:-1])
    )

    system = RowSystem(coupling)
    bwd_x, head_x, tail_x = system.reduce_source(source_x)
    bwd_z, head_z, tail_z = system.reduce_source(second_z)
    parts = rows
    payload = jnp.stack(
        [
            jnp.stack(system.head + [head_x, head_z]),
            jnp.stack(system.tail + [tail_x, tail_z]),
        ],
        1,
    )
    payload = to_solver(payload, parts)
    received = lax.all_to_all(payload, "row", split_axis=0, concat_axis=0, tiled=True)
    width = received.shape[-1]
    received = jnp.transpose(received, (1, 0, 2, 3)).reshape((5, parts * 2, width))
    answer = reduced_solve(received[:3], received[3:], True)
    back = lax.all_to_all(answer, "row", split_axis=0, concat_axis=0, tiled=True)
    bounds = from_solver(back, count_z, count_x)
    half_ex_rows = system.expand(bwd_x, bounds[0], bounds[1])
    half_ex_e = jnp.stack([bounds[6]] + half_ex_rows + [bounds[4]])
    next_ez_rows = system.expand(bwd_z, bounds[2], bounds[3])
    next_ez = jnp.stack(next_ez_rows)
    next_ez_e = jnp.stack(next_ez_rows + [bounds[5]])

    half_hz_e = hz_e[ya, zs] + HALF_STEP * (
        (half_ex_e[1:] - half_ex_e[:-1]) - diff_up(ey_e[ya, zs], 2)
    )
    half_hz_e = jnp.where(inside[ya, zs], half_hz_e, 0.0)

    half_ex = half_ex_e[1 : count_y + 1]
    dy_half_ex = half_ex_e[2:] - half_ex_e[1:-1]
    second_x = keep * half_ex + drive * (
        (half_hz_e[1:] - half_hz_e[:-1])
        - (half_hy_e[:, 1:] - half_hy_e[:, :-1])
        - HALF_STEP * (dx_half_ez[:, 1:] - dx_half_ez[:, :-1])
    )
    second_y = keep * half_ey + drive * (
        (half_hx_e[1:, 1:] - half_hx_e[1:, :-1])
        - diff_down(half_hz_e[1:], 2)
        - HALF_STEP * diff_down(dy_half_ex, 2)
    )

    second_full = gather_cols(second_x, 1)
    next_ex_full = solve_local(second_full, coup_full[1:], 1)
    padded = jnp.pad(next_ex_full, ((0, 0), (0, 1), (0, 0)))
    next_ex_e = lax.dynamic_slice_in_dim(padded, col_index * count_z, count_z + 1, axis=1)
    next_ex = next_ex_e[:, :-1]

    next_ey = solve_local(second_y, coupling, 2)

    next_hx = half_hx_e[1:, 1:] + HALF_STEP * (
        dz_ey_own[1:] - (next_ez_e[1:] - next_ez_e[:-1])
    )
    next_hy = half_hy_e[:, 1:] + HALF_STEP * (
        dx_half_ez[:, 1:] - (next_ex_e[:, 1:] - next_ex_e[:, :-1])
    )
    next_hz = half_hz_e[1:] + HALF_STEP * (dy_half_ex - diff_up(next_ey, 2))
    return (next_ex, next_ey, next_ez, next_hx, next_hy, next_hz)


def solution(mesh):
    spec = P("row", "col", None)
    return jax.shard_map(
        on_device,
        mesh=mesh,
        in_specs=(spec,) * 8,
        out_specs=(spec,) * 6,
        check_vma=False,
    )
```

```python
import jax
import jax.numpy as jnp
from jax import lax
from jax.sharding import PartitionSpec as P

HALF_STEP = 30.0


def with_halo(cells, sides, width):
    for axis, dim in sides:
        count = lax.axis_size(axis)
        ends = count - 1
        head = lax.slice_in_dim(cells, 0, width, axis=dim)
        tail = lax.slice_in_dim(cells, cells.shape[dim] - width, cells.shape[dim], axis=dim)
        cells = jnp.concatenate(
            [
                lax.ppermute(tail, axis, [(i, (i + 1) % count) for i in range(ends)]),
                cells,
                lax.ppermute(head, axis, [((i + 1) % count, i) for i in range(ends)]),
            ],
            axis=dim,
        )
    return cells


def shifted(values, stride, line_axis, filler, forward):
    length = values.shape[line_axis]
    padding = jnp.full_like(lax.slice_in_dim(values, 0, stride, axis=line_axis), filler)
    if forward:
        return jnp.concatenate(
            [lax.slice_in_dim(values, stride, length, axis=line_axis), padding], line_axis
        )
    return jnp.concatenate(
        [padding, lax.slice_in_dim(values, 0, length - stride, axis=line_axis)], line_axis
    )


def diff_up(values, line_axis):
    return shifted(values, 1, line_axis, 0.0, True) - values


def diff_down(values, line_axis):
    return values - shifted(values, 1, line_axis, 0.0, False)


def reduce_lines(sub_diag, main_diag, super_diag, source, line_axis):
    length = source.shape[line_axis]
    stride = 1
    while stride < length:
        sub_lo = shifted(sub_diag, stride, line_axis, 0.0, False)
        mid_lo = shifted(main_diag, stride, line_axis, 1.0, False)
        sup_lo = shifted(super_diag, stride, line_axis, 0.0, False)
        src_lo = shifted(source, stride, line_axis, 0.0, False)
        sub_hi = shifted(sub_diag, stride, line_axis, 0.0, True)
        mid_hi = shifted(main_diag, stride, line_axis, 1.0, True)
        sup_hi = shifted(super_diag, stride, line_axis, 0.0, True)
        src_hi = shifted(source, stride, line_axis, 0.0, True)
        ratio_lo = sub_diag / mid_lo
        ratio_hi = super_diag / mid_hi
        sub_diag = -sub_lo * ratio_lo
        super_diag = -sup_hi * ratio_hi
        main_diag = main_diag - sup_lo * ratio_lo - sub_hi * ratio_hi
        source = source - src_lo * ratio_lo - src_hi * ratio_hi
        stride = stride * 2
    return source / main_diag


def line_flags(length, line_axis, rank):
    iota_shape = [1] * rank
    iota_shape[line_axis] = length
    where_line = lax.broadcasted_iota(jnp.int32, tuple(iota_shape), line_axis)
    return (where_line == 0, where_line == length - 1)


def line_system(coupling, is_first, is_final):
    sub_diag = jnp.where(is_first, 0.0, -coupling)
    main_diag = jnp.where(is_first, 1.0 + coupling, 1.0 + 2.0 * coupling)
    super_diag = jnp.where(is_final, 0.0, -coupling)
    return (sub_diag, main_diag, super_diag)


def solve_local(source, coupling, line_axis):
    is_first, is_final = line_flags(source.shape[line_axis], line_axis, source.ndim)
    sub_diag, main_diag, super_diag = line_system(coupling, is_first, is_final)
    return reduce_lines(sub_diag, main_diag, super_diag, source, line_axis)


def inside_mask(count_y, count_z):
    pos_y = (
        lax.axis_index("row") * count_y
        + lax.broadcasted_iota(jnp.int32, (count_y + 2, 1, 1), 0)
        - 1
    )
    pos_z = (
        lax.axis_index("col") * count_z
        + lax.broadcasted_iota(jnp.int32, (1, count_z + 2, 1), 1)
        - 1
    )
    inside = (
        (pos_y >= 0)
        & (pos_y < count_y * lax.axis_size("row"))
        & (pos_z >= 0)
        & (pos_z < count_z * lax.axis_size("col"))
    )
    return inside


class RowSystem:
    def __init__(self, coupling):
        count = coupling.shape[0]
        self.count = count
        row_index = lax.axis_index("row")
        is_first, is_final = line_flags(count, 0, 3)
        is_first = jnp.logical_and(is_first, row_index == 0)
        is_final = jnp.logical_and(is_final, row_index == lax.axis_size("row") - 1)
        sub, main, sup = line_system(coupling, is_first, is_final)
        self.sub, self.main, self.sup = sub, main, sup
        fwd_sub = [None] * count
        fwd_sup = [None] * count
        pivot = [None] * count
        pivot[1] = main[1]
        fwd_sub[1] = sub[1] / main[1]
        fwd_sup[1] = sup[1] / main[1]
        for level in range(2, count - 1):
            pivot[level] = main[level] - sub[level] * fwd_sup[level - 1]
            fwd_sub[level] = -sub[level] * fwd_sub[level - 1] / pivot[level]
            fwd_sup[level] = sup[level] / pivot[level]
        bwd_sub = [None] * count
        bwd_sup = [None] * count
        bwd_sub[count - 2] = fwd_sub[count - 2]
        bwd_sup[count - 2] = fwd_sup[count - 2]
        for level in range(count - 3, 0, -1):
            bwd_sub[level] = fwd_sub[level] - fwd_sup[level] * bwd_sub[level + 1]
            bwd_sup[level] = -fwd_sup[level] * bwd_sup[level + 1]
        last = count - 1
        self.pivot, self.fwd_sub, self.fwd_sup = pivot, fwd_sub, fwd_sup
        self.bwd_sub, self.bwd_sup = bwd_sub, bwd_sup
        self.head = [sub[0], main[0] - sup[0] * bwd_sub[1], -sup[0] * bwd_sup[1]]
        self.tail = [
            -sub[last] * fwd_sub[last - 1],
            main[last] - sub[last] * fwd_sup[last - 1],
            sup[last],
        ]

    def reduce_source(self, source):
        count = self.count
        sub = self.sub
        fwd_src = [None] * count
        fwd_src[1] = source[1] / self.pivot[1]
        for level in range(2, count - 1):
            fwd_src[level] = (source[level] - sub[level] * fwd_src[level - 1]) / self.pivot[level]
        bwd_src = [None] * count
        bwd_src[count - 2] = fwd_src[count - 2]
        for level in range(count - 3, 0, -1):
            bwd_src[level] = fwd_src[level] - self.fwd_sup[level] * bwd_src[level + 1]
        last = count - 1
        head_src = source[0] - self.sup[0] * bwd_src[1]
        tail_src = source[last] - sub[last] * fwd_src[last - 1]
        return bwd_src, head_src, tail_src

    def expand(self, bwd_src, first_vals, final_vals):
        rows = [first_vals]
        for level in range(1, self.count - 1):
            rows.append(
                bwd_src[level] - self.bwd_sub[level] * first_vals - self.bwd_sup[level] * final_vals
            )
        rows.append(final_vals)
        return rows


def to_solver(planes, parts):
    lead = planes.shape[:-2]
    count_z, count_x = planes.shape[-2:]
    per_z = parts // count_z
    width = count_x // per_z
    split = planes.reshape(lead + (count_z, per_z, width))
    rank = len(lead)
    order = (rank, rank + 1) + tuple(range(rank)) + (rank + 2,)
    split = jnp.transpose(split, order)
    return split.reshape((parts,) + lead + (width,))


def from_solver(chunks, count_z, count_x):
    parts, k, width = chunks.shape
    per_z = parts // count_z
    split = chunks.reshape((count_z, per_z, k, width))
    split = jnp.transpose(split, (2, 0, 1, 3))
    return split.reshape((k, count_z, count_x))


def reduced_solve(matrix, rhs, want_prev):
    solved = reduce_lines(matrix[0][None], matrix[1][None], matrix[2][None], rhs, 1)
    parts = solved.shape[1] // 2
    outs = []
    for one in range(solved.shape[0]):
        pairs = solved[one].reshape((parts, 2) + solved.shape[2:])
        heads = pairs[:, 0]
        tails = pairs[:, 1]
        zero = jnp.zeros_like(heads[:1])
        outs += [heads, tails]
    for one in range(solved.shape[0]):
        heads = outs[2 * one]
        outs.append(jnp.concatenate([heads[1:], zero], 0))
    outs.append(jnp.concatenate([zero, outs[1][:-1]], 0))
    return jnp.stack(outs, 1)


def gather_cols(block, axis):
    cols = lax.axis_size("col")
    col_index = lax.axis_index("col")
    got = [block]
    for shift in range(1, cols):
        got.append(lax.ppermute(block, "col", [(i, (i + shift) % cols) for i in range(cols)]))
    pieces = []
    for place in range(cols):
        shift_needed = (col_index - place) % cols
        piece = got[0]
        for shift in range(1, cols):
            piece = jnp.where(shift_needed == shift, got[shift], piece)
        pieces.append(piece)
    return jnp.concatenate(pieces, axis)


def field_halos(fields, y_prev, y_next, z_prev, z_next):
    rows = lax.axis_size("row")
    cols = lax.axis_size("col")
    down_rows = [(i, i + 1) for i in range(rows - 1)]
    up_rows = [(i + 1, i) for i in range(rows - 1)]
    down_cols = [(i, i + 1) for i in range(cols - 1)]
    up_cols = [(i + 1, i) for i in range(cols - 1)]

    def exchange(pieces_of, chosen, pairs, axis):
        moved = lax.ppermute(jnp.stack([pieces_of[k] for k in chosen]), axis, pairs)
        return {k: moved[n] for n, k in enumerate(chosen)}

    from_prev = exchange([f[-1:] for f in fields], y_prev, down_rows, "row")
    from_next = exchange([f[:1] for f in fields], y_next, up_rows, "row")
    ext_y = []
    for k, f in enumerate(fields):
        zero = jnp.zeros_like(f[:1])
        ext_y.append(
            jnp.concatenate([from_prev.get(k, zero), f, from_next.get(k, zero)], 0)
        )
    from_left = exchange([e[:, -1:] for e in ext_y], z_prev, down_cols, "col")
    from_right = exchange([e[:, :1] for e in ext_y], z_next, up_cols, "col")
    ext = []
    for k, e in enumerate(ext_y):
        zero = jnp.zeros_like(e[:, :1])
        ext.append(
            jnp.concatenate([from_left.get(k, zero), e, from_right.get(k, zero)], 1)
        )
    return ext


def on_device(
    efield_x, efield_y, efield_z, hfield_x, hfield_y, hfield_z, permittivity, conductivity
):
    count_y = efield_x.shape[0]
    count_z = efield_x.shape[1]
    count_x = efield_x.shape[2]
    rows = lax.axis_size("row")
    col_index = lax.axis_index("col")

    ext = field_halos(
        [efield_x, efield_y, efield_z, hfield_x, hfield_y, hfield_z, permittivity, conductivity],
        y_prev=(1, 2, 3, 5, 6, 7),
        y_next=(2,),
        z_prev=(0, 2, 3, 4, 6, 7),
        z_next=(0,),
    )
    inside = inside_mask(count_y, count_z)
    ex_e, ey_e, ez_e = ext[0], ext[1], ext[2]
    hx_e, hy_e, hz_e = ext[3], ext[4], ext[5]
    eps_e = jnp.where(inside, ext[6], 1.0)
    sig_e = jnp.where(inside, ext[7], 0.0)
    damping = sig_e * HALF_STEP / (2.0 * eps_e)
    keep_e = (1.0 - damping) / (1.0 + damping)
    drive_e = HALF_STEP / (eps_e * (1.0 + damping))
    coup_e = drive_e * HALF_STEP

    ys = slice(1, count_y + 1)
    zs = slice(1, count_z + 1)
    keep = keep_e[ys, zs]
    drive = drive_e[ys, zs]
    coupling = coup_e[ys, zs]

    dpx_ey = diff_up(ey_e[0 : count_y + 1, zs], 2)
    source_x = keep * efield_x + drive * (
        (hz_e[ys, zs] - hz_e[0:count_y, zs])
        - (hy_e[ys, zs] - hy_e[ys, 0:count_z])
        - HALF_STEP * (dpx_ey[1:] - dpx_ey[:-1])
    )
    ya = slice(0, count_y + 1)
    dpy_ez = ez_e[1 : count_y + 2, 0 : count_z + 1] - ez_e[0 : count_y + 1, 0 : count_z + 1]
    source_y = keep_e[ya, zs] * ey_e[ya, zs] + drive_e[ya, zs] * (
        (hx_e[ya, zs] - hx_e[ya, 0:count_z])
        - diff_down(hz_e[ya, zs], 2)
        - HALF_STEP * (dpy_ez[:, 1:] - dpy_ez[:, :-1])
    )
    za = slice(0, count_z + 1)
    dpz_ex = ex_e[ys, 1 : count_z + 2] - ex_e[ys, 0 : count_z + 1]
    source_z = keep_e[ys, za] * ez_e[ys, za] + drive_e[ys, za] * (
        diff_down(hy_e[ys, za], 2)
        - (hx_e[ys, za] - hx_e[0:count_y, za])
        - HALF_STEP * diff_down(dpz_ex, 2)
    )

    gathered = gather_cols(jnp.stack([source_y, coup_e[ya, zs]]), 2)
    coup_full = gathered[1]
    half_ey_full = solve_local(gathered[0], coup_full, 1)
    pos_y = (
        lax.axis_index("row") * count_y
        + lax.broadcasted_iota(jnp.int32, (count_y + 1, 1, 1), 0)
        - 1
    )
    half_ey_full = jnp.where(pos_y >= 0, half_ey_full, 0.0)
    padded = jnp.pad(half_ey_full, ((0, 0), (1, 1), (0, 0)))
    half_ey_e = lax.dynamic_slice_in_dim(padded, col_index * count_z, count_z + 2, axis=1)

    half_ez_e = solve_local(source_z, coup_e[ys, za], 2)
    half_ez_e = jnp.where(inside[ys, za], half_ez_e, 0.0)

    half_hy_e = hy_e[ys, za] + HALF_STEP * (diff_up(half_ez_e, 2) - dpz_ex)
    half_hy_e = jnp.where(inside[ys, za], half_hy_e, 0.0)
    dz_half_ey = half_ey_e[:, 1:] - half_ey_e[:, :-1]
    half_hx_e = hx_e[ya, za] + HALF_STEP * (dz_half_ey[:, 0 : count_z + 1] - dpy_ez)
    half_hx_e = jnp.where(inside[ya, za], half_hx_e, 0.0)

    half_ey = half_ey_e[1 : count_y + 1, 1 : count_z + 1]
    half_ez = half_ez_e[:, 1:]
    dx_half_ez = diff_up(half_ez_e, 2)
    dz_ey_own = dz_half_ey[:, 1 : count_z + 1]
    second_z = keep * half_ez + drive * (
        diff_down(half_hy_e[:, 1:], 2)
        - (half_hx_e[1:, 1:] - half_hx_e[:-1, 1:])
        - HALF_STEP * (dz_ey_own[1:] - dz_ey_own[:-1])
    )

    system = RowSystem(coupling)
    bwd_x, head_x, tail_x = system.reduce_source(source_x)
    bwd_z, head_z, tail_z = system.reduce_source(second_z)
    parts = rows
    payload = jnp.stack(
        [
            jnp.stack(system.head + [head_x, head_z]),
            jnp.stack(system.tail + [tail_x, tail_z]),
        ],
        1,
    )
    payload = to_solver(payload, parts)
    received = lax.all_to_all(payload, "row", split_axis=0, concat_axis=0, tiled=True)
    width = received.shape[-1]
    received = jnp.transpose(received, (1, 0, 2, 3)).reshape((5, parts * 2, width))
    answer = reduced_solve(received[:3], received[3:], True)
    back = lax.all_to_all(answer, "row", split_axis=0, concat_axis=0, tiled=True)
    bounds = from_solver(back, count_z, count_x)
    half_ex_rows = system.expand(bwd_x, bounds[0], bounds[1])
    half_ex_e = jnp.stack([bounds[6]] + half_ex_rows + [bounds[4]])
    next_ez_rows = system.expand(bwd_z, bounds[2], bounds[3])
    next_ez = jnp.stack(next_ez_rows)
    next_ez_e = jnp.stack(next_ez_rows + [bounds[5]])

    half_hz_e = hz_e[ya, zs] + HALF_STEP * (
        (half_ex_e[1:] - half_ex_e[:-1]) - diff_up(ey_e[ya, zs], 2)
    )
    half_hz_e = jnp.where(inside[ya, zs], half_hz_e, 0.0)

    half_ex = half_ex_e[1 : count_y + 1]
    dy_half_ex = half_ex_e[2:] - half_ex_e[1:-1]
    second_x = keep * half_ex + drive * (
        (half_hz_e[1:] - half_hz_e[:-1])
        - (half_hy_e[:, 1:] - half_hy_e[:, :-1])
        - HALF_STEP * (dx_half_ez[:, 1:] - dx_half_ez[:, :-1])
    )
    second_y = keep * half_ey + drive * (
        (half_hx_e[1:, 1:] - half_hx_e[1:, :-1])
        - diff_down(half_hz_e[1:], 2)
        - HALF_STEP * diff_down(dy_half_ex, 2)
    )

    second_full = gather_cols(second_x, 1)
    next_ex_full = solve_local(second_full, coup_full[1:], 1)
    padded = jnp.pad(next_ex_full, ((0, 0), (0, 1), (0, 0)))
    next_ex_e = lax.dynamic_slice_in_dim(padded, col_index * count_z, count_z + 1, axis=1)
    next_ex = next_ex_e[:, :-1]

    next_ey = solve_local(second_y, coupling, 2)

    next_hx = half_hx_e[1:, 1:] + HALF_STEP * (
        dz_ey_own[1:] - (next_ez_e[1:] - next_ez_e[:-1])
    )
    next_hy = half_hy_e[:, 1:] + HALF_STEP * (
        dx_half_ez[:, 1:] - (next_ex_e[:, 1:] - next_ex_e[:, :-1])
    )
    next_hz = half_hz_e[1:] + HALF_STEP * (dy_half_ex - diff_up(next_ey, 2))
    return (next_ex, next_ey, next_ez, next_hx, next_hy, next_hz)


def solution(mesh):
    spec = P("row", "col", None)
    return jax.shard_map(
        on_device,
        mesh=mesh,
        in_specs=(spec,) * 8,
        out_specs=(spec,) * 6,
        check_vma=False,
    )
```

```python
import functools

import jax
import jax.numpy as jnp
from jax import lax
from jax.sharding import PartitionSpec as P
from jax.experimental import pallas as pl
from jax.experimental.pallas import tpu as pltpu

HALF_STEP = 30.0
INTERPRET = False


def with_halo(cells, sides, width):
    for axis, dim in sides:
        count = lax.axis_size(axis)
        ends = count - 1
        head = lax.slice_in_dim(cells, 0, width, axis=dim)
        tail = lax.slice_in_dim(cells, cells.shape[dim] - width, cells.shape[dim], axis=dim)
        cells = jnp.concatenate(
            [
                lax.ppermute(tail, axis, [(i, (i + 1) % count) for i in range(ends)]),
                cells,
                lax.ppermute(head, axis, [((i + 1) % count, i) for i in range(ends)]),
            ],
            axis=dim,
        )
    return cells


def shifted(values, stride, line_axis, filler, forward):
    length = values.shape[line_axis]
    padding = jnp.full_like(lax.slice_in_dim(values, 0, stride, axis=line_axis), filler)
    if forward:
        return jnp.concatenate(
            [lax.slice_in_dim(values, stride, length, axis=line_axis), padding], line_axis
        )
    return jnp.concatenate(
        [padding, lax.slice_in_dim(values, 0, length - stride, axis=line_axis)], line_axis
    )


def diff_up(values, line_axis):
    return shifted(values, 1, line_axis, 0.0, True) - values


def diff_down(values, line_axis):
    return values - shifted(values, 1, line_axis, 0.0, False)


def reduce_lines(sub_diag, main_diag, super_diag, source, line_axis):
    length = source.shape[line_axis]
    stride = 1
    while stride < length:
        sub_lo = shifted(sub_diag, stride, line_axis, 0.0, False)
        mid_lo = shifted(main_diag, stride, line_axis, 1.0, False)
        sup_lo = shifted(super_diag, stride, line_axis, 0.0, False)
        src_lo = shifted(source, stride, line_axis, 0.0, False)
        sub_hi = shifted(sub_diag, stride, line_axis, 0.0, True)
        mid_hi = shifted(main_diag, stride, line_axis, 1.0, True)
        sup_hi = shifted(super_diag, stride, line_axis, 0.0, True)
        src_hi = shifted(source, stride, line_axis, 0.0, True)
        ratio_lo = sub_diag / mid_lo
        ratio_hi = super_diag / mid_hi
        sub_diag = -sub_lo * ratio_lo
        super_diag = -sup_hi * ratio_hi
        main_diag = main_diag - sup_lo * ratio_lo - sub_hi * ratio_hi
        source = source - src_lo * ratio_lo - src_hi * ratio_hi
        stride = stride * 2
    return source / main_diag


def line_flags(length, line_axis, rank):
    iota_shape = [1] * rank
    iota_shape[line_axis] = length
    where_line = lax.broadcasted_iota(jnp.int32, tuple(iota_shape), line_axis)
    return (where_line == 0, where_line == length - 1)


def line_system(coupling, is_first, is_final):
    sub_diag = jnp.where(is_first, 0.0, -coupling)
    main_diag = jnp.where(is_first, 1.0 + coupling, 1.0 + 2.0 * coupling)
    super_diag = jnp.where(is_final, 0.0, -coupling)
    return (sub_diag, main_diag, super_diag)


def solve_local(source, coupling, line_axis):
    is_first, is_final = line_flags(source.shape[line_axis], line_axis, source.ndim)
    sub_diag, main_diag, super_diag = line_system(coupling, is_first, is_final)
    return reduce_lines(sub_diag, main_diag, super_diag, source, line_axis)


def _line_solve_kernel(source_ref, coupling_ref, out_ref, *, line_axis):
    source = source_ref[...]
    coupling = coupling_ref[...]
    length = source.shape[line_axis]
    where_line = lax.broadcasted_iota(jnp.int32, source.shape, line_axis)
    is_first = where_line == 0
    is_final = where_line == length - 1
    sub_diag = jnp.where(is_first, 0.0, -coupling)
    main_diag = jnp.where(is_first, 1.0 + coupling, 1.0 + 2.0 * coupling)
    super_diag = jnp.where(is_final, 0.0, -coupling)
    stride = 1
    while stride < length:
        has_lo = where_line >= stride
        has_hi = where_line < length - stride

        def lo(values, filler):
            return jnp.where(has_lo, pltpu.roll(values, stride, line_axis), filler)

        def hi(values, filler):
            return jnp.where(has_hi, pltpu.roll(values, length - stride, line_axis), filler)

        sub_lo = lo(sub_diag, 0.0)
        mid_lo = lo(main_diag, 1.0)
        sup_lo = lo(super_diag, 0.0)
        src_lo = lo(source, 0.0)
        sub_hi = hi(sub_diag, 0.0)
        mid_hi = hi(main_diag, 1.0)
        sup_hi = hi(super_diag, 0.0)
        src_hi = hi(source, 0.0)
        ratio_lo = sub_diag / mid_lo
        ratio_hi = super_diag / mid_hi
        sub_diag = -sub_lo * ratio_lo
        super_diag = -sup_hi * ratio_hi
        main_diag = main_diag - sup_lo * ratio_lo - sub_hi * ratio_hi
        source = source - src_lo * ratio_lo - src_hi * ratio_hi
        stride = stride * 2
    out_ref[...] = source / main_diag


def solve_lines(source, coupling, line_axis):
    kernel = functools.partial(_line_solve_kernel, line_axis=line_axis)
    return pl.pallas_call(
        kernel,
        out_shape=jax.ShapeDtypeStruct(source.shape, source.dtype),
        interpret=INTERPRET,
    )(source, coupling)


def inside_mask(count_y, count_z):
    pos_y = (
        lax.axis_index("row") * count_y
        + lax.broadcasted_iota(jnp.int32, (count_y + 2, 1, 1), 0)
        - 1
    )
    pos_z = (
        lax.axis_index("col") * count_z
        + lax.broadcasted_iota(jnp.int32, (1, count_z + 2, 1), 1)
        - 1
    )
    inside = (
        (pos_y >= 0)
        & (pos_y < count_y * lax.axis_size("row"))
        & (pos_z >= 0)
        & (pos_z < count_z * lax.axis_size("col"))
    )
    return inside


class RowSystem:
    def __init__(self, coupling):
        count = coupling.shape[0]
        self.count = count
        row_index = lax.axis_index("row")
        is_first, is_final = line_flags(count, 0, 3)
        is_first = jnp.logical_and(is_first, row_index == 0)
        is_final = jnp.logical_and(is_final, row_index == lax.axis_size("row") - 1)
        sub, main, sup = line_system(coupling, is_first, is_final)
        self.sub, self.main, self.sup = sub, main, sup
        fwd_sub = [None] * count
        fwd_sup = [None] * count
        pivot = [None] * count
        pivot[1] = main[1]
        fwd_sub[1] = sub[1] / main[1]
        fwd_sup[1] = sup[1] / main[1]
        for level in range(2, count - 1):
            pivot[level] = main[level] - sub[level] * fwd_sup[level - 1]
            fwd_sub[level] = -sub[level] * fwd_sub[level - 1] / pivot[level]
            fwd_sup[level] = sup[level] / pivot[level]
        bwd_sub = [None] * count
        bwd_sup = [None] * count
        bwd_sub[count - 2] = fwd_sub[count - 2]
        bwd_sup[count - 2] = fwd_sup[count - 2]
        for level in range(count - 3, 0, -1):
            bwd_sub[level] = fwd_sub[level] - fwd_sup[level] * bwd_sub[level + 1]
            bwd_sup[level] = -fwd_sup[level] * bwd_sup[level + 1]
        last = count - 1
        self.pivot, self.fwd_sub, self.fwd_sup = pivot, fwd_sub, fwd_sup
        self.bwd_sub, self.bwd_sup = bwd_sub, bwd_sup
        self.head = [sub[0], main[0] - sup[0] * bwd_sub[1], -sup[0] * bwd_sup[1]]
        self.tail = [
            -sub[last] * fwd_sub[last - 1],
            main[last] - sub[last] * fwd_sup[last - 1],
            sup[last],
        ]

    def reduce_source(self, source):
        count = self.count
        sub = self.sub
        fwd_src = [None] * count
        fwd_src[1] = source[1] / self.pivot[1]
        for level in range(2, count - 1):
            fwd_src[level] = (source[level] - sub[level] * fwd_src[level - 1]) / self.pivot[level]
        bwd_src = [None] * count
        bwd_src[count - 2] = fwd_src[count - 2]
        for level in range(count - 3, 0, -1):
            bwd_src[level] = fwd_src[level] - self.fwd_sup[level] * bwd_src[level + 1]
        last = count - 1
        head_src = source[0] - self.sup[0] * bwd_src[1]
        tail_src = source[last] - sub[last] * fwd_src[last - 1]
        return bwd_src, head_src, tail_src

    def expand(self, bwd_src, first_vals, final_vals):
        rows = [first_vals]
        for level in range(1, self.count - 1):
            rows.append(
                bwd_src[level] - self.bwd_sub[level] * first_vals - self.bwd_sup[level] * final_vals
            )
        rows.append(final_vals)
        return rows


def to_solver(planes, parts):
    lead = planes.shape[:-2]
    count_z, count_x = planes.shape[-2:]
    per_z = parts // count_z
    width = count_x // per_z
    split = planes.reshape(lead + (count_z, per_z, width))
    rank = len(lead)
    order = (rank, rank + 1) + tuple(range(rank)) + (rank + 2,)
    split = jnp.transpose(split, order)
    return split.reshape((parts,) + lead + (width,))


def from_solver(chunks, count_z, count_x):
    parts, k, width = chunks.shape
    per_z = parts // count_z
    split = chunks.reshape((count_z, per_z, k, width))
    split = jnp.transpose(split, (2, 0, 1, 3))
    return split.reshape((k, count_z, count_x))


def reduced_solve(matrix, rhs, want_prev):
    solved = reduce_lines(matrix[0][None], matrix[1][None], matrix[2][None], rhs, 1)
    parts = solved.shape[1] // 2
    outs = []
    for one in range(solved.shape[0]):
        pairs = solved[one].reshape((parts, 2) + solved.shape[2:])
        heads = pairs[:, 0]
        tails = pairs[:, 1]
        zero = jnp.zeros_like(heads[:1])
        outs += [heads, tails]
    for one in range(solved.shape[0]):
        heads = outs[2 * one]
        outs.append(jnp.concatenate([heads[1:], zero], 0))
    outs.append(jnp.concatenate([zero, outs[1][:-1]], 0))
    return jnp.stack(outs, 1)


def gather_cols(block, axis):
    cols = lax.axis_size("col")
    col_index = lax.axis_index("col")
    got = [block]
    for shift in range(1, cols):
        got.append(lax.ppermute(block, "col", [(i, (i + shift) % cols) for i in range(cols)]))
    pieces = []
    for place in range(cols):
        shift_needed = (col_index - place) % cols
        piece = got[0]
        for shift in range(1, cols):
            piece = jnp.where(shift_needed == shift, got[shift], piece)
        pieces.append(piece)
    return jnp.concatenate(pieces, axis)


def field_halos(fields, y_prev, y_next, z_prev, z_next):
    rows = lax.axis_size("row")
    cols = lax.axis_size("col")
    down_rows = [(i, i + 1) for i in range(rows - 1)]
    up_rows = [(i + 1, i) for i in range(rows - 1)]
    down_cols = [(i, i + 1) for i in range(cols - 1)]
    up_cols = [(i + 1, i) for i in range(cols - 1)]

    def exchange(pieces_of, chosen, pairs, axis):
        moved = lax.ppermute(jnp.stack([pieces_of[k] for k in chosen]), axis, pairs)
        return {k: moved[n] for n, k in enumerate(chosen)}

    from_prev = exchange([f[-1:] for f in fields], y_prev, down_rows, "row")
    from_next = exchange([f[:1] for f in fields], y_next, up_rows, "row")
    ext_y = []
    for k, f in enumerate(fields):
        zero = jnp.zeros_like(f[:1])
        ext_y.append(
            jnp.concatenate([from_prev.get(k, zero), f, from_next.get(k, zero)], 0)
        )
    from_left = exchange([e[:, -1:] for e in ext_y], z_prev, down_cols, "col")
    from_right = exchange([e[:, :1] for e in ext_y], z_next, up_cols, "col")
    ext = []
    for k, e in enumerate(ext_y):
        zero = jnp.zeros_like(e[:, :1])
        ext.append(
            jnp.concatenate([from_left.get(k, zero), e, from_right.get(k, zero)], 1)
        )
    return ext


def on_device(
    efield_x, efield_y, efield_z, hfield_x, hfield_y, hfield_z, permittivity, conductivity
):
    count_y = efield_x.shape[0]
    count_z = efield_x.shape[1]
    count_x = efield_x.shape[2]
    rows = lax.axis_size("row")
    col_index = lax.axis_index("col")

    ext = field_halos(
        [efield_x, efield_y, efield_z, hfield_x, hfield_y, hfield_z, permittivity, conductivity],
        y_prev=(1, 2, 3, 5, 6, 7),
        y_next=(2,),
        z_prev=(0, 2, 3, 4, 6, 7),
        z_next=(0,),
    )
    inside = inside_mask(count_y, count_z)
    ex_e, ey_e, ez_e = ext[0], ext[1], ext[2]
    hx_e, hy_e, hz_e = ext[3], ext[4], ext[5]
    eps_e = jnp.where(inside, ext[6], 1.0)
    sig_e = jnp.where(inside, ext[7], 0.0)
    damping = sig_e * HALF_STEP / (2.0 * eps_e)
    keep_e = (1.0 - damping) / (1.0 + damping)
    drive_e = HALF_STEP / (eps_e * (1.0 + damping))
    coup_e = drive_e * HALF_STEP

    ys = slice(1, count_y + 1)
    zs = slice(1, count_z + 1)
    keep = keep_e[ys, zs]
    drive = drive_e[ys, zs]
    coupling = coup_e[ys, zs]

    dpx_ey = diff_up(ey_e[0 : count_y + 1, zs], 2)
    source_x = keep * efield_x + drive * (
        (hz_e[ys, zs] - hz_e[0:count_y, zs])
        - (hy_e[ys, zs] - hy_e[ys, 0:count_z])
        - HALF_STEP * (dpx_ey[1:] - dpx_ey[:-1])
    )
    ya = slice(0, count_y + 1)
    dpy_ez = ez_e[1 : count_y + 2, 0 : count_z + 1] - ez_e[0 : count_y + 1, 0 : count_z + 1]
    source_y = keep_e[ya, zs] * ey_e[ya, zs] + drive_e[ya, zs] * (
        (hx_e[ya, zs] - hx_e[ya, 0:count_z])
        - diff_down(hz_e[ya, zs], 2)
        - HALF_STEP * (dpy_ez[:, 1:] - dpy_ez[:, :-1])
    )
    za = slice(0, count_z + 1)
    dpz_ex = ex_e[ys, 1 : count_z + 2] - ex_e[ys, 0 : count_z + 1]
    source_z = keep_e[ys, za] * ez_e[ys, za] + drive_e[ys, za] * (
        diff_down(hy_e[ys, za], 2)
        - (hx_e[ys, za] - hx_e[0:count_y, za])
        - HALF_STEP * diff_down(dpz_ex, 2)
    )

    gathered = gather_cols(jnp.stack([source_y, coup_e[ya, zs]]), 2)
    coup_full = gathered[1]
    half_ey_full = solve_lines(gathered[0], coup_full, 1)
    pos_y = (
        lax.axis_index("row") * count_y
        + lax.broadcasted_iota(jnp.int32, (count_y + 1, 1, 1), 0)
        - 1
    )
    half_ey_full = jnp.where(pos_y >= 0, half_ey_full, 0.0)
    padded = jnp.pad(half_ey_full, ((0, 0), (1, 1), (0, 0)))
    half_ey_e = lax.dynamic_slice_in_dim(padded, col_index * count_z, count_z + 2, axis=1)

    half_ez_e = solve_lines(source_z, coup_e[ys, za], 2)
    half_ez_e = jnp.where(inside[ys, za], half_ez_e, 0.0)

    half_hy_e = hy_e[ys, za] + HALF_STEP * (diff_up(half_ez_e, 2) - dpz_ex)
    half_hy_e = jnp.where(inside[ys, za], half_hy_e, 0.0)
    dz_half_ey = half_ey_e[:, 1:] - half_ey_e[:, :-1]
    half_hx_e = hx_e[ya, za] + HALF_STEP * (dz_half_ey[:, 0 : count_z + 1] - dpy_ez)
    half_hx_e = jnp.where(inside[ya, za], half_hx_e, 0.0)

    half_ey = half_ey_e[1 : count_y + 1, 1 : count_z + 1]
    half_ez = half_ez_e[:, 1:]
    dx_half_ez = diff_up(half_ez_e, 2)
    dz_ey_own = dz_half_ey[:, 1 : count_z + 1]
    second_z = keep * half_ez + drive * (
        diff_down(half_hy_e[:, 1:], 2)
        - (half_hx_e[1:, 1:] - half_hx_e[:-1, 1:])
        - HALF_STEP * (dz_ey_own[1:] - dz_ey_own[:-1])
    )

    system = RowSystem(coupling)
    bwd_x, head_x, tail_x = system.reduce_source(source_x)
    bwd_z, head_z, tail_z = system.reduce_source(second_z)
    parts = rows
    payload = jnp.stack(
        [
            jnp.stack(system.head + [head_x, head_z]),
            jnp.stack(system.tail + [tail_x, tail_z]),
        ],
        1,
    )
    payload = to_solver(payload, parts)
    received = lax.all_to_all(payload, "row", split_axis=0, concat_axis=0, tiled=True)
    width = received.shape[-1]
    received = jnp.transpose(received, (1, 0, 2, 3)).reshape((5, parts * 2, width))
    answer = reduced_solve(received[:3], received[3:], True)
    back = lax.all_to_all(answer, "row", split_axis=0, concat_axis=0, tiled=True)
    bounds = from_solver(back, count_z, count_x)
    half_ex_rows = system.expand(bwd_x, bounds[0], bounds[1])
    half_ex_e = jnp.stack([bounds[6]] + half_ex_rows + [bounds[4]])
    next_ez_rows = system.expand(bwd_z, bounds[2], bounds[3])
    next_ez = jnp.stack(next_ez_rows)
    next_ez_e = jnp.stack(next_ez_rows + [bounds[5]])

    half_hz_e = hz_e[ya, zs] + HALF_STEP * (
        (half_ex_e[1:] - half_ex_e[:-1]) - diff_up(ey_e[ya, zs], 2)
    )
    half_hz_e = jnp.where(inside[ya, zs], half_hz_e, 0.0)

    half_ex = half_ex_e[1 : count_y + 1]
    dy_half_ex = half_ex_e[2:] - half_ex_e[1:-1]
    second_x = keep * half_ex + drive * (
        (half_hz_e[1:] - half_hz_e[:-1])
        - (half_hy_e[:, 1:] - half_hy_e[:, :-1])
        - HALF_STEP * (dx_half_ez[:, 1:] - dx_half_ez[:, :-1])
    )
    second_y = keep * half_ey + drive * (
        (half_hx_e[1:, 1:] - half_hx_e[1:, :-1])
        - diff_down(half_hz_e[1:], 2)
        - HALF_STEP * diff_down(dy_half_ex, 2)
    )

    second_full = gather_cols(second_x, 1)
    next_ex_full = solve_lines(second_full, coup_full[1:], 1)
    padded = jnp.pad(next_ex_full, ((0, 0), (0, 1), (0, 0)))
    next_ex_e = lax.dynamic_slice_in_dim(padded, col_index * count_z, count_z + 1, axis=1)
    next_ex = next_ex_e[:, :-1]

    next_ey = solve_lines(second_y, coupling, 2)

    next_hx = half_hx_e[1:, 1:] + HALF_STEP * (
        dz_ey_own[1:] - (next_ez_e[1:] - next_ez_e[:-1])
    )
    next_hy = half_hy_e[:, 1:] + HALF_STEP * (
        dx_half_ez[:, 1:] - (next_ex_e[:, 1:] - next_ex_e[:, :-1])
    )
    next_hz = half_hz_e[1:] + HALF_STEP * (dy_half_ex - diff_up(next_ey, 2))
    return (next_ex, next_ey, next_ez, next_hx, next_hy, next_hz)


def solution(mesh):
    spec = P("row", "col", None)
    return jax.shard_map(
        on_device,
        mesh=mesh,
        in_specs=(spec,) * 8,
        out_specs=(spec,) * 6,
        check_vma=False,
    )
```

```python
import functools

import jax
import jax.numpy as jnp
from jax import lax
from jax.sharding import PartitionSpec as P
from jax.experimental import pallas as pl
from jax.experimental.pallas import tpu as pltpu

HALF_STEP = 30.0
INTERPRET = False


def with_halo(cells, sides, width):
    for axis, dim in sides:
        count = lax.axis_size(axis)
        ends = count - 1
        head = lax.slice_in_dim(cells, 0, width, axis=dim)
        tail = lax.slice_in_dim(cells, cells.shape[dim] - width, cells.shape[dim], axis=dim)
        cells = jnp.concatenate(
            [
                lax.ppermute(tail, axis, [(i, (i + 1) % count) for i in range(ends)]),
                cells,
                lax.ppermute(head, axis, [((i + 1) % count, i) for i in range(ends)]),
            ],
            axis=dim,
        )
    return cells


def shifted(values, stride, line_axis, filler, forward):
    length = values.shape[line_axis]
    padding = jnp.full_like(lax.slice_in_dim(values, 0, stride, axis=line_axis), filler)
    if forward:
        return jnp.concatenate(
            [lax.slice_in_dim(values, stride, length, axis=line_axis), padding], line_axis
        )
    return jnp.concatenate(
        [padding, lax.slice_in_dim(values, 0, length - stride, axis=line_axis)], line_axis
    )


def diff_up(values, line_axis):
    return shifted(values, 1, line_axis, 0.0, True) - values


def diff_down(values, line_axis):
    return values - shifted(values, 1, line_axis, 0.0, False)


def reduce_lines(sub_diag, main_diag, super_diag, source, line_axis):
    length = source.shape[line_axis]
    stride = 1
    while stride < length:
        sub_lo = shifted(sub_diag, stride, line_axis, 0.0, False)
        mid_lo = shifted(main_diag, stride, line_axis, 1.0, False)
        sup_lo = shifted(super_diag, stride, line_axis, 0.0, False)
        src_lo = shifted(source, stride, line_axis, 0.0, False)
        sub_hi = shifted(sub_diag, stride, line_axis, 0.0, True)
        mid_hi = shifted(main_diag, stride, line_axis, 1.0, True)
        sup_hi = shifted(super_diag, stride, line_axis, 0.0, True)
        src_hi = shifted(source, stride, line_axis, 0.0, True)
        ratio_lo = sub_diag / mid_lo
        ratio_hi = super_diag / mid_hi
        sub_diag = -sub_lo * ratio_lo
        super_diag = -sup_hi * ratio_hi
        main_diag = main_diag - sup_lo * ratio_lo - sub_hi * ratio_hi
        source = source - src_lo * ratio_lo - src_hi * ratio_hi
        stride = stride * 2
    return source / main_diag


def line_flags(length, line_axis, rank):
    iota_shape = [1] * rank
    iota_shape[line_axis] = length
    where_line = lax.broadcasted_iota(jnp.int32, tuple(iota_shape), line_axis)
    return (where_line == 0, where_line == length - 1)


def line_system(coupling, is_first, is_final):
    sub_diag = jnp.where(is_first, 0.0, -coupling)
    main_diag = jnp.where(is_first, 1.0 + coupling, 1.0 + 2.0 * coupling)
    super_diag = jnp.where(is_final, 0.0, -coupling)
    return (sub_diag, main_diag, super_diag)


def solve_local(source, coupling, line_axis):
    is_first, is_final = line_flags(source.shape[line_axis], line_axis, source.ndim)
    sub_diag, main_diag, super_diag = line_system(coupling, is_first, is_final)
    return reduce_lines(sub_diag, main_diag, super_diag, source, line_axis)


def _line_solve_kernel(source_ref, coupling_ref, out_ref, *, line_axis):
    source = source_ref[...]
    coupling = coupling_ref[...]
    length = source.shape[line_axis]
    where_line = lax.broadcasted_iota(jnp.int32, source.shape, line_axis)
    is_first = where_line == 0
    is_final = where_line == length - 1
    sub_diag = jnp.where(is_first, 0.0, -coupling)
    main_diag = jnp.where(is_first, 1.0 + coupling, 1.0 + 2.0 * coupling)
    super_diag = jnp.where(is_final, 0.0, -coupling)
    stride = 1
    while stride < length:
        has_lo = where_line >= stride
        has_hi = where_line < length - stride

        def lo(values, filler):
            return jnp.where(has_lo, pltpu.roll(values, stride, line_axis), filler)

        def hi(values, filler):
            return jnp.where(has_hi, pltpu.roll(values, length - stride, line_axis), filler)

        sub_lo = lo(sub_diag, 0.0)
        mid_lo = lo(main_diag, 1.0)
        sup_lo = lo(super_diag, 0.0)
        src_lo = lo(source, 0.0)
        sub_hi = hi(sub_diag, 0.0)
        mid_hi = hi(main_diag, 1.0)
        sup_hi = hi(super_diag, 0.0)
        src_hi = hi(source, 0.0)
        ratio_lo = sub_diag / mid_lo
        ratio_hi = super_diag / mid_hi
        sub_diag = -sub_lo * ratio_lo
        super_diag = -sup_hi * ratio_hi
        main_diag = main_diag - sup_lo * ratio_lo - sub_hi * ratio_hi
        source = source - src_lo * ratio_lo - src_hi * ratio_hi
        stride = stride * 2
    out_ref[...] = source / main_diag


def solve_lines(source, coupling, line_axis):
    kernel = functools.partial(_line_solve_kernel, line_axis=line_axis)
    return pl.pallas_call(
        kernel,
        out_shape=jax.ShapeDtypeStruct(source.shape, source.dtype),
        interpret=INTERPRET,
    )(source, coupling)


def inside_mask(count_y, count_z):
    pos_y = (
        lax.axis_index("row") * count_y
        + lax.broadcasted_iota(jnp.int32, (count_y + 2, 1, 1), 0)
        - 1
    )
    pos_z = (
        lax.axis_index("col") * count_z
        + lax.broadcasted_iota(jnp.int32, (1, count_z + 2, 1), 1)
        - 1
    )
    inside = (
        (pos_y >= 0)
        & (pos_y < count_y * lax.axis_size("row"))
        & (pos_z >= 0)
        & (pos_z < count_z * lax.axis_size("col"))
    )
    return inside


class RowSystem:
    def __init__(self, coupling):
        count = coupling.shape[0]
        self.count = count
        row_index = lax.axis_index("row")
        is_first, is_final = line_flags(count, 0, 3)
        is_first = jnp.logical_and(is_first, row_index == 0)
        is_final = jnp.logical_and(is_final, row_index == lax.axis_size("row") - 1)
        sub, main, sup = line_system(coupling, is_first, is_final)
        self.sub, self.main, self.sup = sub, main, sup
        fwd_sub = [None] * count
        fwd_sup = [None] * count
        pivot = [None] * count
        pivot[1] = main[1]
        fwd_sub[1] = sub[1] / main[1]
        fwd_sup[1] = sup[1] / main[1]
        for level in range(2, count - 1):
            pivot[level] = main[level] - sub[level] * fwd_sup[level - 1]
            fwd_sub[level] = -sub[level] * fwd_sub[level - 1] / pivot[level]
            fwd_sup[level] = sup[level] / pivot[level]
        bwd_sub = [None] * count
        bwd_sup = [None] * count
        bwd_sub[count - 2] = fwd_sub[count - 2]
        bwd_sup[count - 2] = fwd_sup[count - 2]
        for level in range(count - 3, 0, -1):
            bwd_sub[level] = fwd_sub[level] - fwd_sup[level] * bwd_sub[level + 1]
            bwd_sup[level] = -fwd_sup[level] * bwd_sup[level + 1]
        last = count - 1
        self.pivot, self.fwd_sub, self.fwd_sup = pivot, fwd_sub, fwd_sup
        self.bwd_sub, self.bwd_sup = bwd_sub, bwd_sup
        self.head = [sub[0], main[0] - sup[0] * bwd_sub[1], -sup[0] * bwd_sup[1]]
        self.tail = [
            -sub[last] * fwd_sub[last - 1],
            main[last] - sub[last] * fwd_sup[last - 1],
            sup[last],
        ]

    def reduce_source(self, source):
        count = self.count
        sub = self.sub
        fwd_src = [None] * count
        fwd_src[1] = source[1] / self.pivot[1]
        for level in range(2, count - 1):
            fwd_src[level] = (source[level] - sub[level] * fwd_src[level - 1]) / self.pivot[level]
        bwd_src = [None] * count
        bwd_src[count - 2] = fwd_src[count - 2]
        for level in range(count - 3, 0, -1):
            bwd_src[level] = fwd_src[level] - self.fwd_sup[level] * bwd_src[level + 1]
        last = count - 1
        head_src = source[0] - self.sup[0] * bwd_src[1]
        tail_src = source[last] - sub[last] * fwd_src[last - 1]
        return bwd_src, head_src, tail_src

    def expand(self, bwd_src, first_vals, final_vals):
        rows = [first_vals]
        for level in range(1, self.count - 1):
            rows.append(
                bwd_src[level] - self.bwd_sub[level] * first_vals - self.bwd_sup[level] * final_vals
            )
        rows.append(final_vals)
        return rows


def to_solver(planes, parts):
    lead = planes.shape[:-2]
    count_z, count_x = planes.shape[-2:]
    per_z = parts // count_z
    width = count_x // per_z
    split = planes.reshape(lead + (count_z, per_z, width))
    rank = len(lead)
    order = (rank, rank + 1) + tuple(range(rank)) + (rank + 2,)
    split = jnp.transpose(split, order)
    return split.reshape((parts,) + lead + (width,))


def from_solver(chunks, count_z, count_x):
    parts, k, width = chunks.shape
    per_z = parts // count_z
    split = chunks.reshape((count_z, per_z, k, width))
    split = jnp.transpose(split, (2, 0, 1, 3))
    return split.reshape((k, count_z, count_x))


def reduced_solve(matrix, rhs, want_prev):
    solved = reduce_lines(matrix[0][None], matrix[1][None], matrix[2][None], rhs, 1)
    parts = solved.shape[1] // 2
    outs = []
    for one in range(solved.shape[0]):
        pairs = solved[one].reshape((parts, 2) + solved.shape[2:])
        heads = pairs[:, 0]
        tails = pairs[:, 1]
        zero = jnp.zeros_like(heads[:1])
        outs += [heads, tails]
    for one in range(solved.shape[0]):
        heads = outs[2 * one]
        outs.append(jnp.concatenate([heads[1:], zero], 0))
    outs.append(jnp.concatenate([zero, outs[1][:-1]], 0))
    return jnp.stack(outs, 1)


def gather_cols(block, axis):
    cols = lax.axis_size("col")
    col_index = lax.axis_index("col")
    got = [block]
    for shift in range(1, cols):
        got.append(lax.ppermute(block, "col", [(i, (i + shift) % cols) for i in range(cols)]))
    pieces = []
    for place in range(cols):
        shift_needed = (col_index - place) % cols
        piece = got[0]
        for shift in range(1, cols):
            piece = jnp.where(shift_needed == shift, got[shift], piece)
        pieces.append(piece)
    return jnp.concatenate(pieces, axis)


def field_halos(fields, y_prev, y_next, z_prev, z_next, corner_pp, corner_np):
    rows = lax.axis_size("row")
    cols = lax.axis_size("col")
    both = ("row", "col")

    def flat(r, c):
        return r * cols + c

    down_rows = [(i, i + 1) for i in range(rows - 1)]
    up_rows = [(i + 1, i) for i in range(rows - 1)]
    down_cols = [(i, i + 1) for i in range(cols - 1)]
    up_cols = [(i + 1, i) for i in range(cols - 1)]
    diag_pp = [
        (flat(r, c), flat(r + 1, c + 1)) for r in range(rows - 1) for c in range(cols - 1)
    ]
    diag_np = [
        (flat(r + 1, c), flat(r, c + 1)) for r in range(rows - 1) for c in range(cols - 1)
    ]

    def exchange(pieces_of, chosen, pairs, axis):
        if not chosen:
            return {}
        moved = lax.ppermute(jnp.stack([pieces_of(k) for k in chosen]), axis, pairs)
        return {k: moved[n] for n, k in enumerate(chosen)}

    got_yp = exchange(lambda k: fields[k][-1:], y_prev, down_rows, "row")
    got_yn = exchange(lambda k: fields[k][:1], y_next, up_rows, "row")
    got_zp = exchange(lambda k: fields[k][:, -1:], z_prev, down_cols, "col")
    got_zn = exchange(lambda k: fields[k][:, :1], z_next, up_cols, "col")
    got_pp = exchange(lambda k: fields[k][-1:, -1:], corner_pp, diag_pp, both)
    got_np = exchange(lambda k: fields[k][:1, -1:], corner_np, diag_np, both)
    ext = []
    for k, f in enumerate(fields):
        row_zero = jnp.zeros_like(f[:1])
        col_zero = jnp.zeros_like(f[:, :1])
        cell_zero = jnp.zeros_like(f[:1, :1])
        top = jnp.concatenate(
            [got_pp.get(k, cell_zero), got_yp.get(k, row_zero), cell_zero], 1
        )
        middle = jnp.concatenate([got_zp.get(k, col_zero), f, got_zn.get(k, col_zero)], 1)
        bottom = jnp.concatenate(
            [got_np.get(k, cell_zero), got_yn.get(k, row_zero), cell_zero], 1
        )
        ext.append(jnp.concatenate([top, middle, bottom], 0))
    return ext


def on_device(
    efield_x, efield_y, efield_z, hfield_x, hfield_y, hfield_z, permittivity, conductivity
):
    count_y = efield_x.shape[0]
    count_z = efield_x.shape[1]
    count_x = efield_x.shape[2]
    rows = lax.axis_size("row")
    col_index = lax.axis_index("col")

    ext = field_halos(
        [efield_x, efield_y, efield_z, hfield_x, hfield_y, hfield_z, permittivity, conductivity],
        y_prev=(1, 2, 3, 5, 6, 7),
        y_next=(2,),
        z_prev=(0, 2, 3, 4, 6, 7),
        z_next=(0,),
        corner_pp=(2, 3),
        corner_np=(2,),
    )
    inside = inside_mask(count_y, count_z)
    ex_e, ey_e, ez_e = ext[0], ext[1], ext[2]
    hx_e, hy_e, hz_e = ext[3], ext[4], ext[5]
    eps_e = jnp.where(inside, ext[6], 1.0)
    sig_e = jnp.where(inside, ext[7], 0.0)
    damping = sig_e * HALF_STEP / (2.0 * eps_e)
    keep_e = (1.0 - damping) / (1.0 + damping)
    drive_e = HALF_STEP / (eps_e * (1.0 + damping))
    coup_e = drive_e * HALF_STEP

    ys = slice(1, count_y + 1)
    zs = slice(1, count_z + 1)
    keep = keep_e[ys, zs]
    drive = drive_e[ys, zs]
    coupling = coup_e[ys, zs]

    dpx_ey = diff_up(ey_e[0 : count_y + 1, zs], 2)
    source_x = keep * efield_x + drive * (
        (hz_e[ys, zs] - hz_e[0:count_y, zs])
        - (hy_e[ys, zs] - hy_e[ys, 0:count_z])
        - HALF_STEP * (dpx_ey[1:] - dpx_ey[:-1])
    )
    ya = slice(0, count_y + 1)
    dpy_ez = ez_e[1 : count_y + 2, 0 : count_z + 1] - ez_e[0 : count_y + 1, 0 : count_z + 1]
    source_y = keep_e[ya, zs] * ey_e[ya, zs] + drive_e[ya, zs] * (
        (hx_e[ya, zs] - hx_e[ya, 0:count_z])
        - diff_down(hz_e[ya, zs], 2)
        - HALF_STEP * (dpy_ez[:, 1:] - dpy_ez[:, :-1])
    )
    za = slice(0, count_z + 1)
    dpz_ex = ex_e[ys, 1 : count_z + 2] - ex_e[ys, 0 : count_z + 1]
    source_z = keep_e[ys, za] * ez_e[ys, za] + drive_e[ys, za] * (
        diff_down(hy_e[ys, za], 2)
        - (hx_e[ys, za] - hx_e[0:count_y, za])
        - HALF_STEP * diff_down(dpz_ex, 2)
    )

    gathered = gather_cols(jnp.stack([source_y, coup_e[ya, zs]]), 2)
    coup_full = gathered[1]
    half_ey_full = solve_lines(gathered[0], coup_full, 1)
    pos_y = (
        lax.axis_index("row") * count_y
        + lax.broadcasted_iota(jnp.int32, (count_y + 1, 1, 1), 0)
        - 1
    )
    half_ey_full = jnp.where(pos_y >= 0, half_ey_full, 0.0)
    padded = jnp.pad(half_ey_full, ((0, 0), (1, 1), (0, 0)))
    half_ey_e = lax.dynamic_slice_in_dim(padded, col_index * count_z, count_z + 2, axis=1)

    half_ez_e = solve_lines(source_z, coup_e[ys, za], 2)
    half_ez_e = jnp.where(inside[ys, za], half_ez_e, 0.0)

    half_hy_e = hy_e[ys, za] + HALF_STEP * (diff_up(half_ez_e, 2) - dpz_ex)
    half_hy_e = jnp.where(inside[ys, za], half_hy_e, 0.0)
    dz_half_ey = half_ey_e[:, 1:] - half_ey_e[:, :-1]
    half_hx_e = hx_e[ya, za] + HALF_STEP * (dz_half_ey[:, 0 : count_z + 1] - dpy_ez)
    half_hx_e = jnp.where(inside[ya, za], half_hx_e, 0.0)

    half_ey = half_ey_e[1 : count_y + 1, 1 : count_z + 1]
    half_ez = half_ez_e[:, 1:]
    dx_half_ez = diff_up(half_ez_e, 2)
    dz_ey_own = dz_half_ey[:, 1 : count_z + 1]
    second_z = keep * half_ez + drive * (
        diff_down(half_hy_e[:, 1:], 2)
        - (half_hx_e[1:, 1:] - half_hx_e[:-1, 1:])
        - HALF_STEP * (dz_ey_own[1:] - dz_ey_own[:-1])
    )

    system = RowSystem(coupling)
    bwd_x, head_x, tail_x = system.reduce_source(source_x)
    bwd_z, head_z, tail_z = system.reduce_source(second_z)
    parts = rows
    payload = jnp.stack(
        [
            jnp.stack(system.head + [head_x, head_z]),
            jnp.stack(system.tail + [tail_x, tail_z]),
        ],
        1,
    )
    payload = to_solver(payload, parts)
    received = lax.all_to_all(payload, "row", split_axis=0, concat_axis=0, tiled=True)
    width = received.shape[-1]
    received = jnp.transpose(received, (1, 0, 2, 3)).reshape((5, parts * 2, width))
    answer = reduced_solve(received[:3], received[3:], True)
    back = lax.all_to_all(answer, "row", split_axis=0, concat_axis=0, tiled=True)
    bounds = from_solver(back, count_z, count_x)
    half_ex_rows = system.expand(bwd_x, bounds[0], bounds[1])
    half_ex_e = jnp.stack([bounds[6]] + half_ex_rows + [bounds[4]])
    next_ez_rows = system.expand(bwd_z, bounds[2], bounds[3])
    next_ez = jnp.stack(next_ez_rows)
    next_ez_e = jnp.stack(next_ez_rows + [bounds[5]])

    half_hz_e = hz_e[ya, zs] + HALF_STEP * (
        (half_ex_e[1:] - half_ex_e[:-1]) - diff_up(ey_e[ya, zs], 2)
    )
    half_hz_e = jnp.where(inside[ya, zs], half_hz_e, 0.0)

    half_ex = half_ex_e[1 : count_y + 1]
    dy_half_ex = half_ex_e[2:] - half_ex_e[1:-1]
    second_x = keep * half_ex + drive * (
        (half_hz_e[1:] - half_hz_e[:-1])
        - (half_hy_e[:, 1:] - half_hy_e[:, :-1])
        - HALF_STEP * (dx_half_ez[:, 1:] - dx_half_ez[:, :-1])
    )
    second_y = keep * half_ey + drive * (
        (half_hx_e[1:, 1:] - half_hx_e[1:, :-1])
        - diff_down(half_hz_e[1:], 2)
        - HALF_STEP * diff_down(dy_half_ex, 2)
    )

    second_full = gather_cols(second_x, 1)
    next_ex_full = solve_lines(second_full, coup_full[1:], 1)
    padded = jnp.pad(next_ex_full, ((0, 0), (0, 1), (0, 0)))
    next_ex_e = lax.dynamic_slice_in_dim(padded, col_index * count_z, count_z + 1, axis=1)
    next_ex = next_ex_e[:, :-1]

    next_ey = solve_lines(second_y, coupling, 2)

    next_hx = half_hx_e[1:, 1:] + HALF_STEP * (
        dz_ey_own[1:] - (next_ez_e[1:] - next_ez_e[:-1])
    )
    next_hy = half_hy_e[:, 1:] + HALF_STEP * (
        dx_half_ez[:, 1:] - (next_ex_e[:, 1:] - next_ex_e[:, :-1])
    )
    next_hz = half_hz_e[1:] + HALF_STEP * (dy_half_ex - diff_up(next_ey, 2))
    return (next_ex, next_ey, next_ez, next_hx, next_hy, next_hz)


def solution(mesh):
    spec = P("row", "col", None)
    return jax.shard_map(
        on_device,
        mesh=mesh,
        in_specs=(spec,) * 8,
        out_specs=(spec,) * 6,
        check_vma=False,
    )
```
